512 devices in a mesh: ctx: 64 (over z_lo, x, core), tp: 8 (over y, z_hi).
Axes of the slice: x: 4, y: 4, z: 16 (z_hi: 2, z_lo: 8; z = z_hi * 8 + z_lo), core: 2. Of those that a mesh axis runs over, the one named last changes fastest.
Arguments:
- u_query: bfloat16 [8192, 4096], P('ctx', 'tp'), may hold values from -6 to 6
- u_key: bfloat16 [8192, 4096], P('ctx', 'tp'), may hold values from -6 to 6
- u_value: bfloat16 [8192, 4096], P('ctx', 'tp'), may hold values from -6 to 6
- short_filter: float32 [3, 7, 4096], P(None, None, 'tp'), may hold values from -2 to 2
- decay_rate: float32 [256, 16], P('tp'), may hold values from 3.6621094e-05 to 0.0333333333
- residue: float32 [256, 16], P('tp'), may hold values from -1.8 to 1.8
- grad_out: bfloat16 [8192, 4096], P('ctx', 'tp'), may hold values from -6 to 6
Outputs:
- mixer_out: bfloat16 [8192, 4096], P('ctx', 'tp')
- grad_query: bfloat16 [8192, 4096], P('ctx', 'tp')
- grad_key: bfloat16 [8192, 4096], P('ctx', 'tp')
- grad_value: bfloat16 [8192, 4096], P('ctx', 'tp')
The draws below stay inside these ranges and needn't reach their ends.
All inputs are finite; a program needn't handle non-finite values.
Results may differ from the reference program's by a relative error of at most 0.0076.
Values may be sent and summed in bfloat16 or wider, within the bound.
No kernel may reach another device: no remote copies, remote signals or barrier semaphores. Data moves between devices by JAX's collectives and lax.ppermute only.
A program may use at most 128 MiB of HBM per device.

```python
import math
import jax
import jax.numpy as jnp
from jax import lax

D = 4096
GROUP = 16
ORDER = 16
SHORT = 7
TOK_DEV = 128
TOKENS = 8192
G = 256


def draw_decay_rate(key, part):
    key_rate = jax.random.fold_in(key, 1)
    slow_top = math.log(math.log(10.0) / TOKENS)
    fast_top = math.log(1.0 / 30.0)
    log_rates = jax.random.uniform(key_rate, (G, ORDER), jnp.float32, slow_top, fast_top)
    return jnp.exp(log_rates)


def block_levels(rng, shape, cuts, low, high):
    level = 1.0
    for axis_at, parts in cuts:
        draws = jax.random.uniform(jax.random.fold_in(jax.random.fold_in(rng, 6), axis_at), (parts,), jnp.float32, low / len(cuts), high / len(cuts))
        level = level * jnp.repeat(jnp.exp(draws), shape[axis_at] // parts).reshape((-1,) + (1,) * (len(shape) - 1 - axis_at))
    return level


def bell_draw(stream_key, extent, spread, reach, cuts=(), dtype=jnp.bfloat16):
    loudness = block_levels(stream_key, extent, cuts, -0.22, 0.18) if cuts else 1.0
    array = jax.random.normal(stream_key, extent, jnp.float32) * spread * loudness
    return jnp.minimum(jnp.maximum(array, -reach), reach).astype(dtype)


def setup_inputs(seed: int = 0) -> dict:
    streams_of = jax.random.split(jax.random.key(seed), 8)
    u_query = bell_draw(streams_of[0], (TOKENS, D), 1.0, 6.0, ((0, 64), (1, 8)))
    u_key = bell_draw(streams_of[1], (TOKENS, D), 1.0, 6.0, ((0, 64), (1, 8)))
    u_value = bell_draw(streams_of[2], (TOKENS, D), 1.0, 6.0, ((0, 64), (1, 8)))
    short_filter = bell_draw(streams_of[3], (3, SHORT, D), SHORT ** -0.5, 2.0, ((2, 8),), jnp.float32)
    decay_rate = draw_decay_rate(jax.random.fold_in(streams_of[7], 71), 0)
    residue = bell_draw(streams_of[5], (G, ORDER), 0.3, 1.8, ((0, 8),), jnp.float32)
    grad_out = bell_draw(streams_of[6], (TOKENS, D), 1.0, 6.0, ((0, 64), (1, 8)))
    return dict(u_query=u_query, u_key=u_key, u_value=u_value, short_filter=short_filter, decay_rate=decay_rate, residue=residue, grad_out=grad_out)


precise = lax.Precision.HIGHEST

def rounded(values):
    return lax.optimization_barrier(values.astype(jnp.bfloat16))

def modal_tables(rate_rows, residue, block_len):
    lag_steps = jnp.arange(block_len).astype(jnp.float32)
    powers = jnp.exp(-rate_rows[:, :, None] * lag_steps)
    weights = residue * jnp.sqrt(-jnp.expm1(-2.0 * rate_rows))
    impulse = jnp.einsum('gm,gmk->gk', weights, powers, precision=precise)
    return (weights, powers, impulse)

def short_forward(inputs, filter_taps):
    length = inputs.shape[0]
    padded = jnp.concatenate([jnp.zeros((SHORT - 1, inputs.shape[1]), jnp.float32), inputs.astype(jnp.float32)], axis=0)
    summed = jnp.zeros(inputs.shape, jnp.float32)
    for offset in range(SHORT):
        summed = summed + filter_taps[offset] * padded[SHORT - 1 - offset:SHORT - 1 - offset + length]
    return summed

def short_backward(grad_rows, filter_taps):
    length = grad_rows.shape[0]
    padded = jnp.concatenate([grad_rows.astype(jnp.float32), jnp.zeros((SHORT - 1, grad_rows.shape[1]), jnp.float32)], axis=0)
    summed = jnp.zeros(grad_rows.shape, jnp.float32)
    for offset in range(SHORT):
        summed = summed + filter_taps[offset] * padded[offset:offset + length]
    return summed

def long_conv(signal, decay_rate, residue, backward):
    block_len = TOK_DEV
    groups = D // GROUP
    weights, powers, impulse = modal_tables(decay_rate, residue, block_len)
    lag_grid = (jnp.arange(block_len)[:, None] - jnp.arange(block_len)[None, :]).astype(jnp.int32)
    toeplitz = jnp.where(lag_grid[None] >= 0, impulse[:, jnp.clip(lag_grid, 0, block_len - 1)], 0.0)
    step_factor = jnp.exp(-decay_rate)[:, :, None]
    block_factor = jnp.exp(-decay_rate * block_len)[:, :, None]
    if backward:
        lead_rows = weights[:, :, None] * powers[:, :, ::-1] * step_factor
        sweep = powers
    else:
        lead_rows = weights[:, :, None] * powers * step_factor
        sweep = powers[:, :, ::-1]
    pieces = signal.astype(jnp.float32).reshape(TOKENS // block_len, block_len, groups, GROUP)

    def advance(carried_state, piece_rows):
        if backward:
            local_part = jnp.einsum('gts,tgc->sgc', toeplitz, piece_rows, precision=precise)
        else:
            local_part = jnp.einsum('gts,sgc->tgc', toeplitz, piece_rows, precision=precise)
        carried_part = jnp.einsum('gmt,gmc->tgc', lead_rows, carried_state, precision=precise)
        new_state = block_factor * carried_state + jnp.einsum('gms,sgc->gmc', sweep, piece_rows, precision=precise)
        return (new_state, (local_part + carried_part).reshape(block_len, groups * GROUP))
    start_state = jnp.zeros((groups, ORDER, GROUP), jnp.float32)
    ignored, outputs = lax.scan(advance, start_state, pieces, reverse=backward)
    return outputs.reshape(TOKENS, D)

def reference(u_query, u_key, u_value, short_filter, decay_rate, residue, grad_out):
    q_short = rounded(short_forward(u_query, short_filter[0]))
    k_short = rounded(short_forward(u_key, short_filter[1]))
    v_short = rounded(short_forward(u_value, short_filter[2]))
    product = rounded(k_short.astype(jnp.float32) * v_short.astype(jnp.float32))
    conv_out = rounded(long_conv(product, decay_rate, residue, False))
    mixer_out = (q_short.astype(jnp.float32) * conv_out.astype(jnp.float32)).astype(jnp.bfloat16)
    grad_qshort = rounded(grad_out.astype(jnp.float32) * conv_out.astype(jnp.float32))
    grad_conv = rounded(grad_out.astype(jnp.float32) * q_short.astype(jnp.float32))
    grad_prod = rounded(long_conv(grad_conv, decay_rate, residue, True))
    grad_kshort = rounded(grad_prod.astype(jnp.float32) * v_short.astype(jnp.float32))
    grad_vshort = rounded(grad_prod.astype(jnp.float32) * k_short.astype(jnp.float32))
    grad_query = short_backward(grad_qshort, short_filter[0]).astype(jnp.bfloat16)
    grad_key = short_backward(grad_kshort, short_filter[1]).astype(jnp.bfloat16)
    grad_value = short_backward(grad_vshort, short_filter[2]).astype(jnp.bfloat16)
    return (mixer_out, grad_query, grad_key, grad_value)
```

```python
import jax
import jax.numpy as jnp
from jax import lax
from jax.sharding import PartitionSpec as P

GROUP = 16
SHORT = 7


precise = lax.Precision.HIGHEST


def from_behind(value, axis, steps):
    count = lax.axis_size(axis)
    leading, last = (max(0, -steps), min(count, count - steps))
    return lax.ppermute(value, axis, [(source, source + steps) for source in range(leading, last)])


def rounded(values):
    return lax.optimization_barrier(values.astype(jnp.bfloat16))


def short_causal(prior_rows, inputs, filter_taps):
    length = inputs.shape[0]
    padded = jnp.concatenate([prior_rows.astype(jnp.float32), inputs.astype(jnp.float32)], axis=0)
    summed = jnp.zeros(inputs.shape, jnp.float32)
    for offset in range(SHORT):
        summed = (
            summed + filter_taps[offset] * padded[SHORT - 1 - offset : SHORT - 1 - offset + length]
        )
    return summed


def short_reverse(grad_rows, next_rows, filter_taps):
    length = grad_rows.shape[0]
    padded = jnp.concatenate([grad_rows.astype(jnp.float32), next_rows.astype(jnp.float32)], axis=0)
    summed = jnp.zeros(grad_rows.shape, jnp.float32)
    for offset in range(SHORT):
        summed = summed + filter_taps[offset] * padded[offset : offset + length]
    return summed


def split_dot(spec, table, values):
    high = table.astype(jnp.bfloat16)
    low = (table - high.astype(jnp.float32)).astype(jnp.bfloat16)
    lhs = jnp.einsum(spec, high, values, preferred_element_type=jnp.float32)
    return lhs + jnp.einsum(spec, low, values, preferred_element_type=jnp.float32)


def modal_scan(local_state, decay_step, axis, forward):
    count = lax.axis_size(axis)
    entering = jnp.zeros_like(local_state)
    window = local_state
    shift = 1
    while shift < count:
        if forward:
            pairs = [(source, source + shift) for source in range(count - shift)]
        else:
            pairs = [(source, source - shift) for source in range(shift, count)]
        arrived = lax.ppermute(window, axis, pairs)
        entering = entering + jnp.exp(-decay_step * (shift - 1)) * arrived
        if shift * 2 < count:
            window = window + jnp.exp(-decay_step * shift) * arrived
        shift *= 2
    return entering


def shards(u_query, u_key, u_value, short_filter, decay_rate, residue, grad_out):
    block_len, channels = u_query.shape
    group_count = channels // GROUP
    rim_rows = jnp.stack(
        [
            u_query[block_len - SHORT + 1 :],
            u_key[block_len - SHORT + 1 :],
            u_value[block_len - SHORT + 1 :],
        ]
    )
    before = from_behind(rim_rows, "ctx", 1)
    q_short = rounded(short_causal(before[0], u_query, short_filter[0]))
    k_short = rounded(short_causal(before[1], u_key, short_filter[1]))
    v_short = rounded(short_causal(before[2], u_value, short_filter[2]))
    product = rounded(k_short.astype(jnp.float32) * v_short.astype(jnp.float32))
    grad_conv = rounded(grad_out.astype(jnp.float32) * q_short.astype(jnp.float32))

    rates = decay_rate
    weights = residue * jnp.sqrt(-jnp.expm1(-2.0 * rates))
    lags = jnp.arange(block_len + 1).astype(jnp.float32)
    powers = jnp.exp(-rates[:, :, None] * lags)
    centred = jnp.arange(block_len).astype(jnp.float32) - block_len // 2
    falling = weights[:, None, :] * jnp.exp(-centred[None, :, None] * rates[:, None, :])
    rising = jnp.exp(centred[None, None, :] * rates[:, :, None])
    toeplitz = jnp.einsum("gtm,gms->gts", falling, rising, precision=precise)
    lower = jnp.arange(block_len)[:, None] >= jnp.arange(block_len)[None, :]
    toeplitz = jnp.where(lower[None], toeplitz, 0.0)

    signal = product.reshape(block_len, group_count, GROUP)
    cotangent = grad_conv.reshape(block_len, group_count, GROUP)
    end_state = split_dot("gms,sgc->gmc", powers[:, :, block_len - 1 :: -1], signal)
    start_state = split_dot("gms,sgc->gmc", powers[:, :, :block_len], cotangent)
    decay_step = (rates * block_len)[:, :, None]
    entering = modal_scan(end_state, decay_step, "ctx", True)
    leaving = modal_scan(start_state, decay_step, "ctx", False)

    local_conv = split_dot("gts,sgc->tgc", toeplitz, signal)
    local_grad = split_dot("gts,tgc->sgc", toeplitz, cotangent)
    lead_fwd = weights[:, None, :] * jnp.swapaxes(powers[:, :, 1:], 1, 2)
    lead_bwd = weights[:, None, :] * jnp.swapaxes(powers[:, :, block_len:0:-1], 1, 2)
    carried_conv = jnp.einsum("gtm,gmc->tgc", lead_fwd, entering, precision=precise)
    carried_grad = jnp.einsum("gsm,gmc->sgc", lead_bwd, leaving, precision=precise)
    conv_out = rounded((local_conv + carried_conv).reshape(block_len, channels))
    grad_prod = rounded((local_grad + carried_grad).reshape(block_len, channels))

    mixer_out = (q_short.astype(jnp.float32) * conv_out.astype(jnp.float32)).astype(jnp.bfloat16)
    grad_qshort = rounded(grad_out.astype(jnp.float32) * conv_out.astype(jnp.float32))
    grad_kshort = rounded(grad_prod.astype(jnp.float32) * v_short.astype(jnp.float32))
    grad_vshort = rounded(grad_prod.astype(jnp.float32) * k_short.astype(jnp.float32))
    head_rows = jnp.stack(
        [grad_qshort[: SHORT - 1], grad_kshort[: SHORT - 1], grad_vshort[: SHORT - 1]]
    )
    next_rows = from_behind(head_rows, "ctx", -1)
    grad_query = short_reverse(grad_qshort, next_rows[0], short_filter[0]).astype(jnp.bfloat16)
    grad_key = short_reverse(grad_kshort, next_rows[1], short_filter[1]).astype(jnp.bfloat16)
    grad_value = short_reverse(grad_vshort, next_rows[2], short_filter[2]).astype(jnp.bfloat16)
    return (mixer_out, grad_query, grad_key, grad_value)


def solution(mesh):
    return jax.shard_map(
        shards,
        mesh=mesh,
        in_specs=(
            P("ctx", "tp"),
            P("ctx", "tp"),
            P("ctx", "tp"),
            P(None, None, "tp"),
            P("tp", None),
            P("tp", None),
            P("ctx", "tp"),
        ),
        out_specs=(P("ctx", "tp"), P("ctx", "tp"), P("ctx", "tp"), P("ctx", "tp")),
        check_vma=False,
    )
```

```python
import math

import jax
import jax.numpy as jnp
from jax import lax
from jax.sharding import Mesh, PartitionSpec as P

GROUP = 16
SHORT = 7
INNER = 8


precise = lax.Precision.HIGHEST


def from_behind(value, axis, steps):
    count = lax.axis_size(axis)
    leading, last = (max(0, -steps), min(count, count - steps))
    return lax.ppermute(value, axis, [(source, source + steps) for source in range(leading, last)])


def rounded(values):
    return lax.optimization_barrier(values.astype(jnp.bfloat16))


def short_causal(prior_rows, inputs, filter_taps):
    length = inputs.shape[0]
    padded = jnp.concatenate([prior_rows.astype(jnp.float32), inputs.astype(jnp.float32)], axis=0)
    summed = jnp.zeros(inputs.shape, jnp.float32)
    for offset in range(SHORT):
        summed = (
            summed + filter_taps[offset] * padded[SHORT - 1 - offset : SHORT - 1 - offset + length]
        )
    return summed


def short_reverse(grad_rows, next_rows, filter_taps):
    length = grad_rows.shape[0]
    padded = jnp.concatenate([grad_rows.astype(jnp.float32), next_rows.astype(jnp.float32)], axis=0)
    summed = jnp.zeros(grad_rows.shape, jnp.float32)
    for offset in range(SHORT):
        summed = summed + filter_taps[offset] * padded[offset : offset + length]
    return summed


def split_dot(spec, table, values):
    high = lax.reduce_precision(table, exponent_bits=8, mantissa_bits=7)
    low = (table - high).astype(jnp.bfloat16)
    lhs = jnp.einsum(spec, high.astype(jnp.bfloat16), values, preferred_element_type=jnp.float32)
    return lhs + jnp.einsum(spec, low, values, preferred_element_type=jnp.float32)


def cube_scan(tot_fwd, tot_bwd, unit_decay, axis, size, index):
    pre_fwd = jnp.zeros_like(tot_fwd)
    pre_bwd = jnp.zeros_like(tot_bwd)
    shift = 1
    while shift < size:
        pairs = [(source, source ^ shift) for source in range(size)]
        got = lax.ppermute(jnp.stack([tot_fwd, tot_bwd]), axis, pairs)
        upper = (index & shift) != 0
        offset = (index % shift).astype(jnp.float32)
        span = jnp.exp(-unit_decay * shift)
        pre_fwd = jnp.where(upper, pre_fwd + jnp.exp(-unit_decay * offset) * got[0], pre_fwd)
        pre_bwd = jnp.where(
            upper, pre_bwd, pre_bwd + jnp.exp(-unit_decay * (shift - 1 - offset)) * got[1]
        )
        tot_fwd = jnp.where(upper, span * got[0] + tot_fwd, span * tot_fwd + got[0])
        tot_bwd = jnp.where(upper, got[1] + span * tot_bwd, tot_bwd + span * got[1])
        shift *= 2
    return pre_fwd, tot_fwd, pre_bwd, tot_bwd


def shards(inner, u_query, u_key, u_value, short_filter, decay_rate, residue, grad_out):
    block_len, channels = u_query.shape
    group_count = channels // GROUP
    rim_rows = jnp.stack(
        [
            u_query[block_len - SHORT + 1 :],
            u_key[block_len - SHORT + 1 :],
            u_value[block_len - SHORT + 1 :],
        ]
    )
    before = from_behind(rim_rows, ("zl", "xc"), 1)
    q_short = rounded(short_causal(before[0], u_query, short_filter[0]))
    k_short = rounded(short_causal(before[1], u_key, short_filter[1]))
    v_short = rounded(short_causal(before[2], u_value, short_filter[2]))
    product = rounded(k_short.astype(jnp.float32) * v_short.astype(jnp.float32))
    grad_conv = rounded(grad_out.astype(jnp.float32) * q_short.astype(jnp.float32))

    rates = decay_rate
    weights = residue * jnp.sqrt(-jnp.expm1(-2.0 * rates))
    lags = jnp.arange(block_len + 1).astype(jnp.float32)
    powers = jnp.exp(-rates[:, :, None] * lags)
    centred = jnp.arange(block_len).astype(jnp.float32) - block_len // 2
    falling = weights[:, None, :] * jnp.exp(-centred[None, :, None] * rates[:, None, :])
    rising = jnp.exp(centred[None, None, :] * rates[:, :, None])
    toeplitz = jnp.einsum("gtm,gms->gts", falling, rising, precision=precise)
    lower = jnp.arange(block_len)[:, None] >= jnp.arange(block_len)[None, :]
    toeplitz = jnp.where(lower[None], toeplitz, 0.0)

    signal = product.reshape(block_len, group_count, GROUP)
    cotangent = grad_conv.reshape(block_len, group_count, GROUP)
    end_state = split_dot("gms,sgc->gmc", powers[:, :, block_len - 1 :: -1], signal)
    start_state = split_dot("gms,sgc->gmc", powers[:, :, :block_len], cotangent)
    decay_step = (rates * block_len)[:, :, None]
    member = lax.axis_index("xc")
    pre_fwd, group_fwd, pre_bwd, group_bwd = cube_scan(
        end_state, start_state, decay_step, "xc", inner, member
    )
    outer_fwd, _, outer_bwd, _ = cube_scan(
        group_fwd, group_bwd, decay_step * inner, "zl", lax.axis_size("zl"), lax.axis_index("zl")
    )
    place = member.astype(jnp.float32)
    entering = pre_fwd + jnp.exp(-decay_step * place) * outer_fwd
    leaving = pre_bwd + jnp.exp(-decay_step * (inner - 1 - place)) * outer_bwd

    local_conv = split_dot("gts,sgc->tgc", toeplitz, signal)
    local_grad = split_dot("gts,tgc->sgc", toeplitz, cotangent)
    lead_fwd = weights[:, None, :] * jnp.swapaxes(powers[:, :, 1:], 1, 2)
    lead_bwd = weights[:, None, :] * jnp.swapaxes(powers[:, :, block_len:0:-1], 1, 2)
    carried_conv = jnp.einsum("gtm,gmc->tgc", lead_fwd, entering, precision=precise)
    carried_grad = jnp.einsum("gsm,gmc->sgc", lead_bwd, leaving, precision=precise)
    conv_out = rounded((local_conv + carried_conv).reshape(block_len, channels))
    grad_prod = rounded((local_grad + carried_grad).reshape(block_len, channels))

    mixer_out = (q_short.astype(jnp.float32) * conv_out.astype(jnp.float32)).astype(jnp.bfloat16)
    grad_qshort = rounded(grad_out.astype(jnp.float32) * conv_out.astype(jnp.float32))
    grad_kshort = rounded(grad_prod.astype(jnp.float32) * v_short.astype(jnp.float32))
    grad_vshort = rounded(grad_prod.astype(jnp.float32) * k_short.astype(jnp.float32))
    head_rows = jnp.stack(
        [grad_qshort[: SHORT - 1], grad_kshort[: SHORT - 1], grad_vshort[: SHORT - 1]]
    )
    next_rows = from_behind(head_rows, ("zl", "xc"), -1)
    grad_query = short_reverse(grad_qshort, next_rows[0], short_filter[0]).astype(jnp.bfloat16)
    grad_key = short_reverse(grad_kshort, next_rows[1], short_filter[1]).astype(jnp.bfloat16)
    grad_value = short_reverse(grad_vshort, next_rows[2], short_filter[2]).astype(jnp.bfloat16)
    return (mixer_out, grad_query, grad_key, grad_value)


def solution(mesh):
    ctx_count = mesh.shape["ctx"]
    inner = math.gcd(INNER, ctx_count)
    grid = Mesh(
        mesh.devices.reshape(ctx_count // inner, inner, mesh.shape["tp"]), ("zl", "xc", "tp")
    )
    rows = P(("zl", "xc"), "tp")
    return jax.shard_map(
        lambda *arrays: shards(inner, *arrays),
        mesh=grid,
        in_specs=(rows, rows, rows, P(None, None, "tp"), P("tp", None), P("tp", None), rows),
        out_specs=(rows, rows, rows, rows),
        check_vma=False,
    )
```

```python
import math

import jax
import jax.numpy as jnp
from jax import lax
from jax.sharding import Mesh, PartitionSpec as P

GROUP = 16
SHORT = 7
INNER = 8


precise = lax.Precision.HIGHEST


def from_behind(value, axis, steps):
    count = lax.axis_size(axis)
    leading, last = (max(0, -steps), min(count, count - steps))
    return lax.ppermute(value, axis, [(source, source + steps) for source in range(leading, last)])


def rounded(values):
    return lax.optimization_barrier(values.astype(jnp.bfloat16))


def short_causal(prior_rows, inputs, filter_taps):
    length = inputs.shape[0]
    padded = jnp.concatenate([prior_rows.astype(jnp.float32), inputs.astype(jnp.float32)], axis=0)
    summed = jnp.zeros(inputs.shape, jnp.float32)
    for offset in range(SHORT):
        summed = (
            summed + filter_taps[offset] * padded[SHORT - 1 - offset : SHORT - 1 - offset + length]
        )
    return summed


def short_reverse(grad_rows, next_rows, filter_taps):
    length = grad_rows.shape[0]
    padded = jnp.concatenate([grad_rows.astype(jnp.float32), next_rows.astype(jnp.float32)], axis=0)
    summed = jnp.zeros(grad_rows.shape, jnp.float32)
    for offset in range(SHORT):
        summed = summed + filter_taps[offset] * padded[offset : offset + length]
    return summed


def split_dot(spec, table, values):
    high = lax.reduce_precision(table, exponent_bits=8, mantissa_bits=7)
    low = (table - high).astype(jnp.bfloat16)
    lhs = jnp.einsum(spec, high.astype(jnp.bfloat16), values, preferred_element_type=jnp.float32)
    return lhs + jnp.einsum(spec, low, values, preferred_element_type=jnp.float32)


def cube_scan(tot_fwd, tot_bwd, unit_decay, axis, size, index):
    pre_fwd = jnp.zeros_like(tot_fwd)
    pre_bwd = jnp.zeros_like(tot_bwd)
    shift = 1
    while shift < size:
        pairs = [(source, source ^ shift) for source in range(size)]
        got = lax.ppermute(jnp.stack([tot_fwd, tot_bwd]), axis, pairs)
        upper = (index & shift) != 0
        offset = (index % shift).astype(jnp.float32)
        span = jnp.exp(-unit_decay * shift)
        pre_fwd = jnp.where(upper, pre_fwd + jnp.exp(-unit_decay * offset) * got[0], pre_fwd)
        pre_bwd = jnp.where(
            upper, pre_bwd, pre_bwd + jnp.exp(-unit_decay * (shift - 1 - offset)) * got[1]
        )
        tot_fwd = jnp.where(upper, span * got[0] + tot_fwd, span * tot_fwd + got[0])
        tot_bwd = jnp.where(upper, got[1] + span * tot_bwd, tot_bwd + span * got[1])
        shift *= 2
    return pre_fwd, tot_fwd, pre_bwd, tot_bwd


def shards(inner, u_query, u_key, u_value, short_filter, decay_rate, residue, grad_out):
    block_len, channels = u_query.shape
    group_count = channels // GROUP
    rim_rows = jnp.stack(
        [
            u_query[block_len - SHORT + 1 :],
            u_key[block_len - SHORT + 1 :],
            u_value[block_len - SHORT + 1 :],
        ]
    )
    before = from_behind(rim_rows, ("zl", "xc"), 1)
    q_short = rounded(short_causal(before[0], u_query, short_filter[0]))
    k_short = rounded(short_causal(before[1], u_key, short_filter[1]))
    v_short = rounded(short_causal(before[2], u_value, short_filter[2]))
    product = rounded(k_short.astype(jnp.float32) * v_short.astype(jnp.float32))
    grad_conv = rounded(grad_out.astype(jnp.float32) * q_short.astype(jnp.float32))

    rates = decay_rate
    weights = residue * jnp.sqrt(-jnp.expm1(-2.0 * rates))
    lags = jnp.arange(block_len + 1).astype(jnp.float32)
    powers = jnp.exp(-rates[:, :, None] * lags)
    centred = jnp.arange(block_len).astype(jnp.float32) - block_len // 2
    falling = weights[:, None, :] * jnp.exp(-centred[None, :, None] * rates[:, None, :])
    rising = jnp.exp(centred[None, None, :] * rates[:, :, None])
    toeplitz = jnp.einsum("gtm,gms->gts", falling, rising, precision=precise)
    lower = jnp.arange(block_len)[:, None] >= jnp.arange(block_len)[None, :]
    toeplitz = jnp.where(lower[None], toeplitz, 0.0)

    signal = product.reshape(block_len, group_count, GROUP)
    cotangent = grad_conv.reshape(block_len, group_count, GROUP)
    order = rates.shape[1]
    owner = (jnp.arange(channels) // GROUP)[None, :] == jnp.arange(group_count)[:, None]
    owner = owner.astype(jnp.float32)

    def own_block(full):
        return (full.reshape(group_count, order, channels) * owner[:, None, :]).sum(0)

    def spread(state):
        return (state[None] * owner[:, None, :]).reshape(group_count * order, channels)

    end_rows = powers[:, :, block_len - 1 :: -1].reshape(group_count * order, block_len)
    start_rows = powers[:, :, :block_len].reshape(group_count * order, block_len)
    end_state = own_block(split_dot("ks,sc->kc", end_rows, product))
    start_state = own_block(split_dot("ks,sc->kc", start_rows, grad_conv))
    decay_step = jnp.repeat(rates.T, GROUP, axis=1) * block_len
    member = lax.axis_index("xc")
    pre_fwd, group_fwd, pre_bwd, group_bwd = cube_scan(
        end_state, start_state, decay_step, "xc", inner, member
    )
    outer_fwd, _, outer_bwd, _ = cube_scan(
        group_fwd, group_bwd, decay_step * inner, "zl", lax.axis_size("zl"), lax.axis_index("zl")
    )
    place = member.astype(jnp.float32)
    entering = pre_fwd + jnp.exp(-decay_step * place) * outer_fwd
    leaving = pre_bwd + jnp.exp(-decay_step * (inner - 1 - place)) * outer_bwd

    local_conv = split_dot("gts,sgc->tgc", toeplitz, signal).reshape(block_len, channels)
    local_grad = split_dot("gts,tgc->sgc", toeplitz, cotangent).reshape(block_len, channels)
    lead_fwd = (weights[:, :, None] * powers[:, :, 1:]).reshape(group_count * order, block_len)
    lead_bwd = (weights[:, :, None] * powers[:, :, block_len:0:-1]).reshape(
        group_count * order, block_len
    )
    carried_conv = jnp.einsum("kt,kc->tc", lead_fwd, spread(entering), precision=precise)
    carried_grad = jnp.einsum("ks,kc->sc", lead_bwd, spread(leaving), precision=precise)
    conv_out = rounded(local_conv + carried_conv)
    grad_prod = rounded(local_grad + carried_grad)

    mixer_out = (q_short.astype(jnp.float32) * conv_out.astype(jnp.float32)).astype(jnp.bfloat16)
    grad_qshort = rounded(grad_out.astype(jnp.float32) * conv_out.astype(jnp.float32))
    grad_kshort = rounded(grad_prod.astype(jnp.float32) * v_short.astype(jnp.float32))
    grad_vshort = rounded(grad_prod.astype(jnp.float32) * k_short.astype(jnp.float32))
    head_rows = jnp.stack(
        [grad_qshort[: SHORT - 1], grad_kshort[: SHORT - 1], grad_vshort[: SHORT - 1]]
    )
    next_rows = from_behind(head_rows, ("zl", "xc"), -1)
    grad_query = short_reverse(grad_qshort, next_rows[0], short_filter[0]).astype(jnp.bfloat16)
    grad_key = short_reverse(grad_kshort, next_rows[1], short_filter[1]).astype(jnp.bfloat16)
    grad_value = short_reverse(grad_vshort, next_rows[2], short_filter[2]).astype(jnp.bfloat16)
    return (mixer_out, grad_query, grad_key, grad_value)


def solution(mesh):
    ctx_count = mesh.shape["ctx"]
    inner = math.gcd(INNER, ctx_count)
    grid = Mesh(
        mesh.devices.reshape(ctx_count // inner, inner, mesh.shape["tp"]), ("zl", "xc", "tp")
    )
    rows = P(("zl", "xc"), "tp")
    return jax.shard_map(
        lambda *arrays: shards(inner, *arrays),
        mesh=grid,
        in_specs=(rows, rows, rows, P(None, None, "tp"), P("tp", None), P("tp", None), rows),
        out_specs=(rows, rows, rows, rows),
        check_vma=False,
    )
```

```python
import math

import jax
import jax.numpy as jnp
from jax import lax
from jax.sharding import Mesh, PartitionSpec as P

GROUP = 16
SHORT = 7
INNER = 8


precise = lax.Precision.HIGHEST


def from_behind(value, axis, steps):
    count = lax.axis_size(axis)
    leading, last = (max(0, -steps), min(count, count - steps))
    return lax.ppermute(value, axis, [(source, source + steps) for source in range(leading, last)])


def rounded(values):
    return lax.optimization_barrier(values.astype(jnp.bfloat16))


def short_causal(prior_rows, inputs, filter_taps):
    length = inputs.shape[0]
    padded = jnp.concatenate([prior_rows.astype(jnp.float32), inputs.astype(jnp.float32)], axis=0)
    summed = jnp.zeros(inputs.shape, jnp.float32)
    for offset in range(SHORT):
        summed = (
            summed + filter_taps[offset] * padded[SHORT - 1 - offset : SHORT - 1 - offset + length]
        )
    return summed


def short_reverse(grad_rows, next_rows, filter_taps):
    length = grad_rows.shape[0]
    padded = jnp.concatenate([grad_rows.astype(jnp.float32), next_rows.astype(jnp.float32)], axis=0)
    summed = jnp.zeros(grad_rows.shape, jnp.float32)
    for offset in range(SHORT):
        summed = summed + filter_taps[offset] * padded[offset : offset + length]
    return summed


def split_dot(spec, table, values):
    high = lax.reduce_precision(table, exponent_bits=8, mantissa_bits=7)
    low = (table - high).astype(jnp.bfloat16)
    lhs = jnp.einsum(spec, high.astype(jnp.bfloat16), values, preferred_element_type=jnp.float32)
    return lhs + jnp.einsum(spec, low, values, preferred_element_type=jnp.float32)


def cube_coefficients(size, index):
    terms = []
    shift = 1
    while shift < size:
        offset = (index % shift).astype(jnp.float32)
        terms += [jnp.float32(shift), offset, shift - 1 - offset]
        shift *= 2
    return terms


def cube_scan(tot_fwd, tot_bwd, factors, axis, size, index):
    pre_fwd = jnp.zeros_like(tot_fwd)
    pre_bwd = jnp.zeros_like(tot_bwd)
    shift = 1
    step = 0
    while shift < size:
        pairs = [(source, source ^ shift) for source in range(size)]
        got = lax.ppermute(jnp.stack([tot_fwd, tot_bwd]), axis, pairs)
        upper = (index & shift) != 0
        span, lead, trail = factors[step], factors[step + 1], factors[step + 2]
        pre_fwd = jnp.where(upper, pre_fwd + lead * got[0], pre_fwd)
        pre_bwd = jnp.where(upper, pre_bwd, pre_bwd + trail * got[1])
        tot_fwd = jnp.where(upper, span * got[0] + tot_fwd, span * tot_fwd + got[0])
        tot_bwd = jnp.where(upper, got[1] + span * tot_bwd, tot_bwd + span * got[1])
        shift *= 2
        step += 3
    return pre_fwd, tot_fwd, pre_bwd, tot_bwd


def shards(inner, u_query, u_key, u_value, short_filter, decay_rate, residue, grad_out):
    block_len, channels = u_query.shape
    group_count = channels // GROUP
    rim_rows = jnp.stack(
        [
            u_query[block_len - SHORT + 1 :],
            u_key[block_len - SHORT + 1 :],
            u_value[block_len - SHORT + 1 :],
        ]
    )
    before = from_behind(rim_rows, ("zl", "xc"), 1)
    q_short = rounded(short_causal(before[0], u_query, short_filter[0]))
    k_short = rounded(short_causal(before[1], u_key, short_filter[1]))
    v_short = rounded(short_causal(before[2], u_value, short_filter[2]))
    product = rounded(k_short.astype(jnp.float32) * v_short.astype(jnp.float32))
    grad_conv = rounded(grad_out.astype(jnp.float32) * q_short.astype(jnp.float32))

    rates = decay_rate
    weights = residue * jnp.sqrt(-jnp.expm1(-2.0 * rates))
    lags = jnp.arange(block_len + 1).astype(jnp.float32)
    powers = jnp.exp(-rates[:, :, None] * lags)
    centred = jnp.arange(block_len).astype(jnp.float32) - block_len // 2
    falling = weights[:, None, :] * jnp.exp(-centred[None, :, None] * rates[:, None, :])
    rising = jnp.exp(centred[None, None, :] * rates[:, :, None])
    toeplitz = jnp.einsum("gtm,gms->gts", falling, rising, precision=precise)
    lower = jnp.arange(block_len)[:, None] >= jnp.arange(block_len)[None, :]
    toeplitz = jnp.where(lower[None], toeplitz, 0.0)

    signal = product.reshape(block_len, group_count, GROUP)
    cotangent = grad_conv.reshape(block_len, group_count, GROUP)
    order = rates.shape[1]
    owner = (jnp.arange(channels) // GROUP)[None, :] == jnp.arange(group_count)[:, None]
    owner = owner.astype(jnp.float32)

    def own_block(full):
        return (full.reshape(group_count, order, channels) * owner[:, None, :]).sum(0)

    def spread(state):
        return (state[None] * owner[:, None, :]).reshape(group_count * order, channels)

    end_rows = powers[:, :, block_len - 1 :: -1].reshape(group_count * order, block_len)
    start_rows = powers[:, :, :block_len].reshape(group_count * order, block_len)
    end_state = own_block(split_dot("ks,sc->kc", end_rows, product))
    start_state = own_block(split_dot("ks,sc->kc", start_rows, grad_conv))
    decay_step = jnp.repeat(rates.T, GROUP, axis=1) * block_len
    member = lax.axis_index("xc")
    outer = lax.axis_size("zl")
    band = lax.axis_index("zl")
    place = member.astype(jnp.float32)
    inner_terms = cube_coefficients(inner, member)
    outer_terms = [inner * term for term in cube_coefficients(outer, band)]
    terms = jnp.stack(inner_terms + outer_terms + [place, inner - 1 - place])
    factors = jnp.exp(-decay_step[None] * terms[:, None, None])
    pre_fwd, group_fwd, pre_bwd, group_bwd = cube_scan(
        end_state, start_state, factors, "xc", inner, member
    )
    outer_fwd, _, outer_bwd, _ = cube_scan(
        group_fwd, group_bwd, factors[len(inner_terms) :], "zl", outer, band
    )
    entering = pre_fwd + factors[-2] * outer_fwd
    leaving = pre_bwd + factors[-1] * outer_bwd

    local_conv = split_dot("gts,sgc->tgc", toeplitz, signal).reshape(block_len, channels)
    local_grad = split_dot("gts,tgc->sgc", toeplitz, cotangent).reshape(block_len, channels)
    lead_fwd = (weights[:, :, None] * powers[:, :, 1:]).reshape(group_count * order, block_len)
    lead_bwd = (weights[:, :, None] * powers[:, :, block_len:0:-1]).reshape(
        group_count * order, block_len
    )
    carried_conv = jnp.einsum("kt,kc->tc", lead_fwd, spread(entering), precision=precise)
    carried_grad = jnp.einsum("ks,kc->sc", lead_bwd, spread(leaving), precision=precise)
    conv_out = rounded(local_conv + carried_conv)
    grad_prod = rounded(local_grad + carried_grad)

    mixer_out = (q_short.astype(jnp.float32) * conv_out.astype(jnp.float32)).astype(jnp.bfloat16)
    grad_qshort = rounded(grad_out.astype(jnp.float32) * conv_out.astype(jnp.float32))
    grad_kshort = rounded(grad_prod.astype(jnp.float32) * v_short.astype(jnp.float32))
    grad_vshort = rounded(grad_prod.astype(jnp.float32) * k_short.astype(jnp.float32))
    head_rows = jnp.stack(
        [grad_qshort[: SHORT - 1], grad_kshort[: SHORT - 1], grad_vshort[: SHORT - 1]]
    )
    next_rows = from_behind(head_rows, ("zl", "xc"), -1)
    grad_query = short_reverse(grad_qshort, next_rows[0], short_filter[0]).astype(jnp.bfloat16)
    grad_key = short_reverse(grad_kshort, next_rows[1], short_filter[1]).astype(jnp.bfloat16)
    grad_value = short_reverse(grad_vshort, next_rows[2], short_filter[2]).astype(jnp.bfloat16)
    return (mixer_out, grad_query, grad_key, grad_value)


def solution(mesh):
    ctx_count = mesh.shape["ctx"]
    inner = math.gcd(INNER, ctx_count)
    grid = Mesh(
        mesh.devices.reshape(ctx_count // inner, inner, mesh.shape["tp"]), ("zl", "xc", "tp")
    )
    rows = P(("zl", "xc"), "tp")
    return jax.shard_map(
        lambda *arrays: shards(inner, *arrays),
        mesh=grid,
        in_specs=(rows, rows, rows, P(None, None, "tp"), P("tp", None), P("tp", None), rows),
        out_specs=(rows, rows, rows, rows),
        check_vma=False,
    )
```

```python
import math

import jax
import jax.numpy as jnp
from jax import lax
from jax.sharding import Mesh, PartitionSpec as P

GROUP = 16
SHORT = 7
INNER = 8


precise = lax.Precision.HIGHEST


def from_behind(value, axis, steps):
    count = lax.axis_size(axis)
    leading, last = (max(0, -steps), min(count, count - steps))
    return lax.ppermute(value, axis, [(source, source + steps) for source in range(leading, last)])


def rounded(values):
    return lax.optimization_barrier(values.astype(jnp.bfloat16))


def short_causal(prior_rows, inputs, filter_taps):
    length = inputs.shape[0]
    padded = jnp.concatenate([prior_rows.astype(jnp.float32), inputs.astype(jnp.float32)], axis=0)
    summed = jnp.zeros(inputs.shape, jnp.float32)
    for offset in range(SHORT):
        summed = (
            summed + filter_taps[offset] * padded[SHORT - 1 - offset : SHORT - 1 - offset + length]
        )
    return summed


def short_reverse(grad_rows, next_rows, filter_taps):
    length = grad_rows.shape[0]
    padded = jnp.concatenate([grad_rows.astype(jnp.float32), next_rows.astype(jnp.float32)], axis=0)
    summed = jnp.zeros(grad_rows.shape, jnp.float32)
    for offset in range(SHORT):
        summed = summed + filter_taps[offset] * padded[offset : offset + length]
    return summed


def split_dot(spec, table, values):
    high = lax.reduce_precision(table, exponent_bits=8, mantissa_bits=7)
    low = (table - high).astype(jnp.bfloat16)
    lhs = jnp.einsum(spec, high.astype(jnp.bfloat16), values, preferred_element_type=jnp.float32)
    return lhs + jnp.einsum(spec, low, values, preferred_element_type=jnp.float32)


def cube_coefficients(size, index):
    terms = []
    shift = 1
    while shift < size:
        offset = (index % shift).astype(jnp.float32)
        terms += [jnp.float32(shift), offset, shift - 1 - offset]
        shift *= 2
    return terms


def cube_weights(factors, size, index):
    rounds = []
    shift = 1
    step = 0
    while shift < size:
        upper = (index & shift) != 0
        span, lead, trail = factors[step], factors[step + 1], factors[step + 2]
        one = jnp.ones_like(span)
        zero = jnp.zeros_like(span)
        keep = jnp.stack([jnp.where(upper, one, span), jnp.where(upper, span, one)])
        take = jnp.stack([jnp.where(upper, span, one), jnp.where(upper, one, span)])
        add = jnp.stack([jnp.where(upper, lead, zero), jnp.where(upper, zero, trail)])
        rounds.append((keep, take, add))
        shift *= 2
        step += 3
    return rounds


def cube_scan(window, rounds, axis, size):
    entering = jnp.zeros_like(window)
    shift = 1
    for keep, take, add in rounds:
        arrived = lax.ppermute(window, axis, [(source, source ^ shift) for source in range(size)])
        entering = entering + add * arrived
        window = keep * window + take * arrived
        shift *= 2
    return entering, window


def shards(inner, u_query, u_key, u_value, short_filter, decay_rate, residue, grad_out):
    block_len, channels = u_query.shape
    group_count = channels // GROUP
    rim_rows = jnp.stack(
        [
            u_query[block_len - SHORT + 1 :],
            u_key[block_len - SHORT + 1 :],
            u_value[block_len - SHORT + 1 :],
        ]
    )
    before = from_behind(rim_rows, ("zl", "xc"), 1)
    q_short = rounded(short_causal(before[0], u_query, short_filter[0]))
    k_short = rounded(short_causal(before[1], u_key, short_filter[1]))
    v_short = rounded(short_causal(before[2], u_value, short_filter[2]))
    product = rounded(k_short.astype(jnp.float32) * v_short.astype(jnp.float32))
    grad_conv = rounded(grad_out.astype(jnp.float32) * q_short.astype(jnp.float32))

    rates = decay_rate
    weights = residue * jnp.sqrt(-jnp.expm1(-2.0 * rates))
    lags = jnp.arange(block_len + 1).astype(jnp.float32)
    powers = jnp.exp(-rates[:, :, None] * lags)
    centred = jnp.arange(block_len).astype(jnp.float32) - block_len // 2
    falling = weights[:, None, :] * jnp.exp(-centred[None, :, None] * rates[:, None, :])
    rising = jnp.exp(centred[None, None, :] * rates[:, :, None])
    toeplitz = jnp.einsum("gtm,gms->gts", falling, rising, precision=precise)
    lower = jnp.arange(block_len)[:, None] >= jnp.arange(block_len)[None, :]
    toeplitz = jnp.where(lower[None], toeplitz, 0.0)

    signal = product.reshape(block_len, group_count, GROUP)
    cotangent = grad_conv.reshape(block_len, group_count, GROUP)
    order = rates.shape[1]
    owner = (jnp.arange(channels) // GROUP)[None, :] == jnp.arange(group_count)[:, None]
    owner = owner.astype(jnp.float32)

    def own_block(full):
        return (full.reshape(group_count, order, channels) * owner[:, None, :]).sum(0)

    def spread(state):
        return (state[None] * owner[:, None, :]).reshape(group_count * order, channels)

    end_rows = powers[:, :, block_len - 1 :: -1].reshape(group_count * order, block_len)
    start_rows = powers[:, :, :block_len].reshape(group_count * order, block_len)
    end_state = own_block(split_dot("ks,sc->kc", end_rows, product))
    start_state = own_block(split_dot("ks,sc->kc", start_rows, grad_conv))
    decay_step = jnp.repeat(rates.T, GROUP, axis=1) * block_len
    member = lax.axis_index("xc")
    outer = lax.axis_size("zl")
    band = lax.axis_index("zl")
    place = member.astype(jnp.float32)
    inner_terms = cube_coefficients(inner, member)
    outer_terms = [inner * term for term in cube_coefficients(outer, band)]
    terms = jnp.stack(inner_terms + outer_terms + [place, inner - 1 - place])
    factors = jnp.exp(-decay_step[None] * terms[:, None, None])
    inner_rounds = cube_weights(factors, inner, member)
    outer_rounds = cube_weights(factors[len(inner_terms) :], outer, band)
    near, group = cube_scan(jnp.stack([end_state, start_state]), inner_rounds, "xc", inner)
    far, _ = cube_scan(group, outer_rounds, "zl", outer)
    entering = near[0] + factors[-2] * far[0]
    leaving = near[1] + factors[-1] * far[1]

    local_conv = split_dot("gts,sgc->tgc", toeplitz, signal).reshape(block_len, channels)
    local_grad = split_dot("gts,tgc->sgc", toeplitz, cotangent).reshape(block_len, channels)
    lead_fwd = (weights[:, :, None] * powers[:, :, 1:]).reshape(group_count * order, block_len)
    lead_bwd = (weights[:, :, None] * powers[:, :, block_len:0:-1]).reshape(
        group_count * order, block_len
    )
    carried_conv = jnp.einsum("kt,kc->tc", lead_fwd, spread(entering), precision=precise)
    carried_grad = jnp.einsum("ks,kc->sc", lead_bwd, spread(leaving), precision=precise)
    conv_out = rounded(local_conv + carried_conv)
    grad_prod = rounded(local_grad + carried_grad)

    mixer_out = (q_short.astype(jnp.float32) * conv_out.astype(jnp.float32)).astype(jnp.bfloat16)
    grad_qshort = rounded(grad_out.astype(jnp.float32) * conv_out.astype(jnp.float32))
    grad_kshort = rounded(grad_prod.astype(jnp.float32) * v_short.astype(jnp.float32))
    grad_vshort = rounded(grad_prod.astype(jnp.float32) * k_short.astype(jnp.float32))
    head_rows = jnp.stack(
        [grad_qshort[: SHORT - 1], grad_kshort[: SHORT - 1], grad_vshort[: SHORT - 1]]
    )
    next_rows = from_behind(head_rows, ("zl", "xc"), -1)
    grad_query = short_reverse(grad_qshort, next_rows[0], short_filter[0]).astype(jnp.bfloat16)
    grad_key = short_reverse(grad_kshort, next_rows[1], short_filter[1]).astype(jnp.bfloat16)
    grad_value = short_reverse(grad_vshort, next_rows[2], short_filter[2]).astype(jnp.bfloat16)
    return (mixer_out, grad_query, grad_key, grad_value)


def solution(mesh):
    ctx_count = mesh.shape["ctx"]
    inner = math.gcd(INNER, ctx_count)
    grid = Mesh(
        mesh.devices.reshape(ctx_count // inner, inner, mesh.shape["tp"]), ("zl", "xc", "tp")
    )
    rows = P(("zl", "xc"), "tp")
    return jax.shard_map(
        lambda *arrays: shards(inner, *arrays),
        mesh=grid,
        in_specs=(rows, rows, rows, P(None, None, "tp"), P("tp", None), P("tp", None), rows),
        out_specs=(rows, rows, rows, rows),
        check_vma=False,
    )
```

```python
import math

import jax
import jax.numpy as jnp
from jax import lax
from jax.sharding import Mesh, PartitionSpec as P

GROUP = 16
SHORT = 7
INNER = 8


precise = lax.Precision.HIGHEST


def from_behind(value, axis, steps):
    count = lax.axis_size(axis)
    leading, last = (max(0, -steps), min(count, count - steps))
    return lax.ppermute(value, axis, [(source, source + steps) for source in range(leading, last)])


def rounded(values):
    return lax.optimization_barrier(values.astype(jnp.bfloat16))


def short_causal(prior_rows, inputs, filter_taps):
    length = inputs.shape[0]
    padded = jnp.concatenate([prior_rows.astype(jnp.float32), inputs.astype(jnp.float32)], axis=0)
    summed = jnp.zeros(inputs.shape, jnp.float32)
    for offset in range(SHORT):
        summed = (
            summed + filter_taps[offset] * padded[SHORT - 1 - offset : SHORT - 1 - offset + length]
        )
    return summed


def short_reverse(grad_rows, next_rows, filter_taps):
    length = grad_rows.shape[0]
    padded = jnp.concatenate([grad_rows.astype(jnp.float32), next_rows.astype(jnp.float32)], axis=0)
    summed = jnp.zeros(grad_rows.shape, jnp.float32)
    for offset in range(SHORT):
        summed = summed + filter_taps[offset] * padded[offset : offset + length]
    return summed


def split_dot(spec, table, values):
    high = lax.reduce_precision(table, exponent_bits=8, mantissa_bits=7)
    low = (table - high).astype(jnp.bfloat16)
    lhs = jnp.einsum(spec, high.astype(jnp.bfloat16), values, preferred_element_type=jnp.float32)
    return lhs + jnp.einsum(spec, low, values, preferred_element_type=jnp.float32)


def cube_coefficients(size, index):
    terms = []
    shift = 1
    while shift < size:
        offset = (index % shift).astype(jnp.float32)
        terms += [jnp.float32(shift), offset, shift - 1 - offset]
        shift *= 2
    return terms


def cube_weights(factors, size, index):
    rounds = []
    shift = 1
    step = 0
    while shift < size:
        upper = (index & shift) != 0
        span, lead, trail = factors[step], factors[step + 1], factors[step + 2]
        one = jnp.ones_like(span)
        zero = jnp.zeros_like(span)
        keep = jnp.stack([jnp.where(upper, one, span), jnp.where(upper, span, one)])
        take = jnp.stack([jnp.where(upper, span, one), jnp.where(upper, one, span)])
        add = jnp.stack([jnp.where(upper, lead, zero), jnp.where(upper, zero, trail)])
        rounds.append((keep, take, add))
        shift *= 2
        step += 3
    return rounds


def cube_scan(window, rounds, axis, size):
    entering = jnp.zeros_like(window)
    shift = 1
    for keep, take, add in rounds:
        arrived = lax.ppermute(window, axis, [(source, source ^ shift) for source in range(size)])
        entering = entering + add * arrived
        window = keep * window + take * arrived
        shift *= 2
    return entering, window


def shards(inner, u_query, u_key, u_value, short_filter, decay_rate, residue, grad_out):
    block_len, channels = u_query.shape
    group_count = channels // GROUP
    rim_rows = jnp.stack(
        [
            u_query[block_len - SHORT + 1 :],
            u_key[block_len - SHORT + 1 :],
            u_value[block_len - SHORT + 1 :],
        ]
    )
    before = from_behind(rim_rows, ("zl", "xc"), 1)
    q_short = rounded(short_causal(before[0], u_query, short_filter[0]))
    k_short = rounded(short_causal(before[1], u_key, short_filter[1]))
    v_short = rounded(short_causal(before[2], u_value, short_filter[2]))
    product = rounded(k_short.astype(jnp.float32) * v_short.astype(jnp.float32))
    grad_conv = rounded(grad_out.astype(jnp.float32) * q_short.astype(jnp.float32))

    rates = decay_rate
    weights = residue * jnp.sqrt(-jnp.expm1(-2.0 * rates))
    lags = jnp.arange(block_len + 1).astype(jnp.float32)
    powers = jnp.exp(-rates[:, :, None] * lags)
    centred = jnp.arange(block_len).astype(jnp.float32) - block_len // 2
    falling = weights[:, None, :] * jnp.exp(-centred[None, :, None] * rates[:, None, :])
    rising = jnp.exp(centred[None, None, :] * rates[:, :, None])
    toeplitz = jnp.einsum("gtm,gms->gts", falling, rising, precision=precise)
    lower = jnp.arange(block_len)[:, None] >= jnp.arange(block_len)[None, :]
    toeplitz = jnp.where(lower[None], toeplitz, 0.0)

    signal = product.reshape(block_len, group_count, GROUP)
    cotangent = grad_conv.reshape(block_len, group_count, GROUP)
    order = rates.shape[1]
    owner = (jnp.arange(channels) // GROUP)[None, :] == jnp.arange(group_count)[:, None]
    owner = owner.astype(jnp.float32)

    def own_block(full):
        return (full.reshape(group_count, order, channels) * owner[:, None, :]).sum(0)

    def spread(state):
        return (state[None] * owner[:, None, :]).reshape(group_count * order, channels)

    end_rows = powers[:, :, block_len - 1 :: -1].reshape(group_count * order, block_len)
    start_rows = powers[:, :, :block_len].reshape(group_count * order, block_len)
    end_state = own_block(split_dot("ks,sc->kc", end_rows, product))
    start_state = own_block(split_dot("ks,sc->kc", start_rows, grad_conv))
    decay_step = jnp.repeat(rates.T, GROUP, axis=1) * block_len
    member = lax.axis_index("xc")
    outer = lax.axis_size("zl")
    band = lax.axis_index("zl")
    place = member.astype(jnp.float32)
    inner_terms = cube_coefficients(inner, member)
    outer_terms = [inner * term for term in cube_coefficients(outer, band)]
    unit_terms = [place, inner - 1 - place, jnp.float32(1), jnp.float32(-1)]
    terms = jnp.stack(inner_terms + outer_terms + unit_terms)
    factors = jnp.exp(-decay_step[None] * terms[:, None, None])
    inner_rounds = cube_weights(factors, inner, member)
    outer_rounds = cube_weights(factors[len(inner_terms) :], outer, band)
    near, group = cube_scan(jnp.stack([end_state, start_state]), inner_rounds, "xc", inner)
    far, _ = cube_scan(group, outer_rounds, "zl", outer)
    entering = near[0] + factors[-4] * far[0]
    leaving = near[1] + factors[-3] * far[1]

    local_conv = split_dot("gts,sgc->tgc", toeplitz, signal).reshape(block_len, channels)
    local_grad = split_dot("gts,tgc->sgc", toeplitz, cotangent).reshape(block_len, channels)
    lead_fwd = (weights[:, :, None] * powers[:, :, 1:]).reshape(group_count * order, block_len)
    lead_bwd = (weights[:, :, None] * powers[:, :, block_len:0:-1]).reshape(
        group_count * order, block_len
    )
    carried_conv = jnp.einsum("kt,kc->tc", lead_fwd, spread(entering), precision=precise)
    carried_grad = jnp.einsum("ks,kc->sc", lead_bwd, spread(leaving), precision=precise)
    conv_out = rounded(local_conv + carried_conv)
    grad_prod = rounded(local_grad + carried_grad)

    edge = SHORT - 1
    ahead = jnp.concatenate(
        [
            local_conv[:edge],
            local_grad[:edge],
            grad_out[:edge].astype(jnp.float32),
            k_short[:edge].astype(jnp.float32),
            v_short[:edge].astype(jnp.float32),
            start_state,
        ]
    )
    ahead = from_behind(ahead, ("zl", "xc"), -1)
    through = factors[-2] * entering + end_state
    beyond = (leaving - ahead[5 * edge :]) * factors[-1]
    next_conv = rounded(
        ahead[:edge]
        + jnp.einsum("kt,kc->tc", lead_fwd[:, :edge], spread(through), precision=precise)
    )
    next_grad = rounded(
        ahead[edge : 2 * edge]
        + jnp.einsum("ks,kc->sc", lead_bwd[:, :edge], spread(beyond), precision=precise)
    )
    next_rows = (
        rounded(ahead[2 * edge : 3 * edge] * next_conv.astype(jnp.float32)),
        rounded(next_grad.astype(jnp.float32) * ahead[4 * edge : 5 * edge]),
        rounded(next_grad.astype(jnp.float32) * ahead[3 * edge : 4 * edge]),
    )

    mixer_out = (q_short.astype(jnp.float32) * conv_out.astype(jnp.float32)).astype(jnp.bfloat16)
    grad_qshort = rounded(grad_out.astype(jnp.float32) * conv_out.astype(jnp.float32))
    grad_kshort = rounded(grad_prod.astype(jnp.float32) * v_short.astype(jnp.float32))
    grad_vshort = rounded(grad_prod.astype(jnp.float32) * k_short.astype(jnp.float32))
    grad_query = short_reverse(grad_qshort, next_rows[0], short_filter[0]).astype(jnp.bfloat16)
    grad_key = short_reverse(grad_kshort, next_rows[1], short_filter[1]).astype(jnp.bfloat16)
    grad_value = short_reverse(grad_vshort, next_rows[2], short_filter[2]).astype(jnp.bfloat16)
    return (mixer_out, grad_query, grad_key, grad_value)


def solution(mesh):
    ctx_count = mesh.shape["ctx"]
    inner = math.gcd(INNER, ctx_count)
    grid = Mesh(
        mesh.devices.reshape(ctx_count // inner, inner, mesh.shape["tp"]), ("zl", "xc", "tp")
    )
    rows = P(("zl", "xc"), "tp")
    return jax.shard_map(
        lambda *arrays: shards(inner, *arrays),
        mesh=grid,
        in_specs=(rows, rows, rows, P(None, None, "tp"), P("tp", None), P("tp", None), rows),
        out_specs=(rows, rows, rows, rows),
        check_vma=False,
    )
```

```python
import math

import jax
import jax.numpy as jnp
from jax import lax
from jax.sharding import Mesh, PartitionSpec as P

GROUP = 16
SHORT = 7
INNER = 8


precise = lax.Precision.HIGHEST


def from_behind(value, axis, steps):
    count = lax.axis_size(axis)
    leading, last = (max(0, -steps), min(count, count - steps))
    return lax.ppermute(value, axis, [(source, source + steps) for source in range(leading, last)])


def rounded(values):
    return lax.optimization_barrier(values.astype(jnp.bfloat16))


def short_causal(prior_rows, inputs, filter_taps):
    length = inputs.shape[0]
    padded = jnp.concatenate([prior_rows.astype(jnp.float32), inputs.astype(jnp.float32)], axis=0)
    summed = jnp.zeros(inputs.shape, jnp.float32)
    for offset in range(SHORT):
        summed = (
            summed + filter_taps[offset] * padded[SHORT - 1 - offset : SHORT - 1 - offset + length]
        )
    return summed


def short_reverse(grad_rows, next_rows, filter_taps):
    length = grad_rows.shape[0]
    padded = jnp.concatenate([grad_rows.astype(jnp.float32), next_rows.astype(jnp.float32)], axis=0)
    summed = jnp.zeros(grad_rows.shape, jnp.float32)
    for offset in range(SHORT):
        summed = summed + filter_taps[offset] * padded[offset : offset + length]
    return summed


def split_dot(spec, table, values):
    high = lax.reduce_precision(table, exponent_bits=8, mantissa_bits=7)
    low = (table - high).astype(jnp.bfloat16)
    lhs = jnp.einsum(spec, high.astype(jnp.bfloat16), values, preferred_element_type=jnp.float32)
    return lhs + jnp.einsum(spec, low, values, preferred_element_type=jnp.float32)


def cube_coefficients(size, index):
    terms = []
    shift = 1
    while shift < size:
        offset = (index % shift).astype(jnp.float32)
        terms += [jnp.float32(shift), offset, shift - 1 - offset]
        shift *= 2
    return terms


def cube_weights(factors, size, index):
    rounds = []
    shift = 1
    step = 0
    while shift < size:
        upper = (index & shift) != 0
        span, lead, trail = factors[step], factors[step + 1], factors[step + 2]
        one = jnp.ones_like(span)
        zero = jnp.zeros_like(span)
        keep = jnp.stack([jnp.where(upper, one, span), jnp.where(upper, span, one)])
        take = jnp.stack([jnp.where(upper, span, one), jnp.where(upper, one, span)])
        add = jnp.stack([jnp.where(upper, lead, zero), jnp.where(upper, zero, trail)])
        rounds.append((keep, take, add))
        shift *= 2
        step += 3
    return rounds


def cube_scan(window, rounds, axis, size, held):
    entering = jnp.zeros_like(window)
    shift = 1
    for keep, take, add in rounds:
        arrived = lax.ppermute(window, axis, [(source, source ^ shift) for source in range(size)])
        if shift == 1:
            held, arrived = lax.optimization_barrier((held, arrived))
        entering = entering + add * arrived
        window = keep * window + take * arrived
        shift *= 2
    return entering, window, held


def shards(inner, u_query, u_key, u_value, short_filter, decay_rate, residue, grad_out):
    block_len, channels = u_query.shape
    group_count = channels // GROUP
    rim_rows = jnp.stack(
        [
            u_query[block_len - SHORT + 1 :],
            u_key[block_len - SHORT + 1 :],
            u_value[block_len - SHORT + 1 :],
        ]
    )
    before = from_behind(rim_rows, ("zl", "xc"), 1)
    q_short = rounded(short_causal(before[0], u_query, short_filter[0]))
    k_short = rounded(short_causal(before[1], u_key, short_filter[1]))
    v_short = rounded(short_causal(before[2], u_value, short_filter[2]))
    product = rounded(k_short.astype(jnp.float32) * v_short.astype(jnp.float32))
    grad_conv = rounded(grad_out.astype(jnp.float32) * q_short.astype(jnp.float32))

    rates = decay_rate
    weights = residue * jnp.sqrt(-jnp.expm1(-2.0 * rates))
    lags = jnp.arange(block_len + 1).astype(jnp.float32)
    powers = jnp.exp(-rates[:, :, None] * lags)

    signal = product.reshape(block_len, group_count, GROUP)
    cotangent = grad_conv.reshape(block_len, group_count, GROUP)
    order = rates.shape[1]
    owner = (jnp.arange(channels) // GROUP)[None, :] == jnp.arange(group_count)[:, None]
    owner = owner.astype(jnp.float32)

    def own_block(full):
        return (full.reshape(group_count, order, channels) * owner[:, None, :]).sum(0)

    def spread(state):
        return (state[None] * owner[:, None, :]).reshape(group_count * order, channels)

    end_rows = powers[:, :, block_len - 1 :: -1].reshape(group_count * order, block_len)
    start_rows = powers[:, :, :block_len].reshape(group_count * order, block_len)
    end_state = own_block(split_dot("ks,sc->kc", end_rows, product))
    start_state = own_block(split_dot("ks,sc->kc", start_rows, grad_conv))
    decay_step = jnp.repeat(rates.T, GROUP, axis=1) * block_len
    member = lax.axis_index("xc")
    outer = lax.axis_size("zl")
    band = lax.axis_index("zl")
    place = member.astype(jnp.float32)
    inner_terms = cube_coefficients(inner, member)
    outer_terms = [inner * term for term in cube_coefficients(outer, band)]
    unit_terms = [place, inner - 1 - place, jnp.float32(1), jnp.float32(-1)]
    terms = jnp.stack(inner_terms + outer_terms + unit_terms)
    factors = jnp.exp(-decay_step[None] * terms[:, None, None])
    inner_rounds = cube_weights(factors, inner, member)
    outer_rounds = cube_weights(factors[len(inner_terms) :], outer, band)
    near, group, (rates, weights) = cube_scan(
        jnp.stack([end_state, start_state]), inner_rounds, "xc", inner, (rates, weights)
    )
    far, _, _ = cube_scan(group, outer_rounds, "zl", outer, ())
    entering = near[0] + factors[-4] * far[0]
    leaving = near[1] + factors[-3] * far[1]

    centred = jnp.arange(block_len).astype(jnp.float32) - block_len // 2
    falling = weights[:, None, :] * jnp.exp(-centred[None, :, None] * rates[:, None, :])
    rising = jnp.exp(centred[None, None, :] * rates[:, :, None])
    toeplitz = jnp.einsum("gtm,gms->gts", falling, rising, precision=precise)
    lower = jnp.arange(block_len)[:, None] >= jnp.arange(block_len)[None, :]
    toeplitz = jnp.where(lower[None], toeplitz, 0.0)
    local_conv = split_dot("gts,sgc->tgc", toeplitz, signal).reshape(block_len, channels)
    local_grad = split_dot("gts,tgc->sgc", toeplitz, cotangent).reshape(block_len, channels)
    lead_fwd = (weights[:, :, None] * powers[:, :, 1:]).reshape(group_count * order, block_len)
    lead_bwd = (weights[:, :, None] * powers[:, :, block_len:0:-1]).reshape(
        group_count * order, block_len
    )
    carried_conv = jnp.einsum("kt,kc->tc", lead_fwd, spread(entering), precision=precise)
    carried_grad = jnp.einsum("ks,kc->sc", lead_bwd, spread(leaving), precision=precise)
    conv_out = rounded(local_conv + carried_conv)
    grad_prod = rounded(local_grad + carried_grad)

    edge = SHORT - 1
    ahead = jnp.concatenate(
        [
            local_conv[:edge],
            local_grad[:edge],
            grad_out[:edge].astype(jnp.float32),
            k_short[:edge].astype(jnp.float32),
            v_short[:edge].astype(jnp.float32),
            start_state,
        ]
    )
    ahead = from_behind(ahead, ("zl", "xc"), -1)
    through = factors[-2] * entering + end_state
    beyond = (leaving - ahead[5 * edge :]) * factors[-1]
    next_conv = rounded(
        ahead[:edge]
        + jnp.einsum("kt,kc->tc", lead_fwd[:, :edge], spread(through), precision=precise)
    )
    next_grad = rounded(
        ahead[edge : 2 * edge]
        + jnp.einsum("ks,kc->sc", lead_bwd[:, :edge], spread(beyond), precision=precise)
    )
    next_rows = (
        rounded(ahead[2 * edge : 3 * edge] * next_conv.astype(jnp.float32)),
        rounded(next_grad.astype(jnp.float32) * ahead[4 * edge : 5 * edge]),
        rounded(next_grad.astype(jnp.float32) * ahead[3 * edge : 4 * edge]),
    )

    mixer_out = (q_short.astype(jnp.float32) * conv_out.astype(jnp.float32)).astype(jnp.bfloat16)
    grad_qshort = rounded(grad_out.astype(jnp.float32) * conv_out.astype(jnp.float32))
    grad_kshort = rounded(grad_prod.astype(jnp.float32) * v_short.astype(jnp.float32))
    grad_vshort = rounded(grad_prod.astype(jnp.float32) * k_short.astype(jnp.float32))
    grad_query = short_reverse(grad_qshort, next_rows[0], short_filter[0]).astype(jnp.bfloat16)
    grad_key = short_reverse(grad_kshort, next_rows[1], short_filter[1]).astype(jnp.bfloat16)
    grad_value = short_reverse(grad_vshort, next_rows[2], short_filter[2]).astype(jnp.bfloat16)
    return (mixer_out, grad_query, grad_key, grad_value)


def solution(mesh):
    ctx_count = mesh.shape["ctx"]
    inner = math.gcd(INNER, ctx_count)
    grid = Mesh(
        mesh.devices.reshape(ctx_count // inner, inner, mesh.shape["tp"]), ("zl", "xc", "tp")
    )
    rows = P(("zl", "xc"), "tp")
    return jax.shard_map(
        lambda *arrays: shards(inner, *arrays),
        mesh=grid,
        in_specs=(rows, rows, rows, P(None, None, "tp"), P("tp", None), P("tp", None), rows),
        out_specs=(rows, rows, rows, rows),
        check_vma=False,
    )
```

```python
import math

import jax
import jax.numpy as jnp
from jax import lax
from jax.sharding import Mesh, PartitionSpec as P

GROUP = 16
SHORT = 7
INNER = 8


precise = lax.Precision.HIGHEST


def from_behind(value, axis, steps):
    count = lax.axis_size(axis)
    leading, last = (max(0, -steps), min(count, count - steps))
    return lax.ppermute(value, axis, [(source, source + steps) for source in range(leading, last)])


def rounded(values):
    return lax.optimization_barrier(values.astype(jnp.bfloat16))


def short_causal(prior_rows, inputs, filter_taps):
    length = inputs.shape[0]
    padded = jnp.concatenate([prior_rows.astype(jnp.float32), inputs.astype(jnp.float32)], axis=0)
    summed = jnp.zeros(inputs.shape, jnp.float32)
    for offset in range(SHORT):
        summed = (
            summed + filter_taps[offset] * padded[SHORT - 1 - offset : SHORT - 1 - offset + length]
        )
    return summed


def short_reverse(grad_rows, next_rows, filter_taps):
    length = grad_rows.shape[0]
    padded = jnp.concatenate([grad_rows.astype(jnp.float32), next_rows.astype(jnp.float32)], axis=0)
    summed = jnp.zeros(grad_rows.shape, jnp.float32)
    for offset in range(SHORT):
        summed = summed + filter_taps[offset] * padded[offset : offset + length]
    return summed


def split_dot(spec, table, values):
    high = lax.reduce_precision(table, exponent_bits=8, mantissa_bits=7)
    low = (table - high).astype(jnp.bfloat16)
    lhs = jnp.einsum(spec, high.astype(jnp.bfloat16), values, preferred_element_type=jnp.float32)
    return lhs + jnp.einsum(spec, low, values, preferred_element_type=jnp.float32)


def cube_coefficients(size, index):
    terms = []
    shift = 1
    while shift < size:
        offset = (index % shift).astype(jnp.float32)
        terms += [jnp.float32(shift), offset, shift - 1 - offset]
        shift *= 2
    return terms


def cube_weights(factors, size, index):
    rounds = []
    shift = 1
    step = 0
    while shift < size:
        upper = (index & shift) != 0
        span, lead, trail = factors[step], factors[step + 1], factors[step + 2]
        one = jnp.ones_like(span)
        zero = jnp.zeros_like(span)
        keep = jnp.stack([jnp.where(upper, one, span), jnp.where(upper, span, one)])
        take = jnp.stack([jnp.where(upper, span, one), jnp.where(upper, one, span)])
        add = jnp.stack([jnp.where(upper, lead, zero), jnp.where(upper, zero, trail)])
        rounds.append((keep, take, add))
        shift *= 2
        step += 3
    return rounds


def cube_scan(window, rounds, axis, size, held):
    entering = jnp.zeros_like(window)
    shift = 1
    for keep, take, add in rounds:
        arrived = lax.ppermute(window, axis, [(source, source ^ shift) for source in range(size)])
        if shift == 1:
            held, arrived = lax.optimization_barrier((held, arrived))
        entering = entering + add * arrived
        window = keep * window + take * arrived
        shift *= 2
    return entering, window, held


def shards(inner, u_query, u_key, u_value, short_filter, decay_rate, residue, grad_out):
    block_len, channels = u_query.shape
    group_count = channels // GROUP
    rim_rows = jnp.stack(
        [
            u_query[block_len - SHORT + 1 :],
            u_key[block_len - SHORT + 1 :],
            u_value[block_len - SHORT + 1 :],
        ]
    )
    before = from_behind(rim_rows, ("zl", "xc"), 1)
    edge = SHORT - 1
    head_rows = jnp.stack([u_query[:edge], u_key[:edge], u_value[:edge], grad_out[:edge]])
    after = from_behind(head_rows, ("zl", "xc"), -1)
    q_short = rounded(short_causal(before[0], u_query, short_filter[0]))
    k_short = rounded(short_causal(before[1], u_key, short_filter[1]))
    v_short = rounded(short_causal(before[2], u_value, short_filter[2]))
    product = rounded(k_short.astype(jnp.float32) * v_short.astype(jnp.float32))
    grad_conv = rounded(grad_out.astype(jnp.float32) * q_short.astype(jnp.float32))

    rates = decay_rate
    weights = residue * jnp.sqrt(-jnp.expm1(-2.0 * rates))
    lags = jnp.arange(block_len + 1).astype(jnp.float32)
    powers = jnp.exp(-rates[:, :, None] * lags)

    signal = product.reshape(block_len, group_count, GROUP)
    cotangent = grad_conv.reshape(block_len, group_count, GROUP)
    order = rates.shape[1]
    owner = (jnp.arange(channels) // GROUP)[None, :] == jnp.arange(group_count)[:, None]
    owner = owner.astype(jnp.float32)

    def own_block(full):
        return (full.reshape(group_count, order, channels) * owner[:, None, :]).sum(0)

    def spread(state):
        return (state[None] * owner[:, None, :]).reshape(group_count * order, channels)

    end_rows = powers[:, :, block_len - 1 :: -1].reshape(group_count * order, block_len)
    start_rows = powers[:, :, :block_len].reshape(group_count * order, block_len)
    end_state = own_block(split_dot("ks,sc->kc", end_rows, product))
    start_state = own_block(split_dot("ks,sc->kc", start_rows, grad_conv))
    decay_step = jnp.repeat(rates.T, GROUP, axis=1) * block_len
    member = lax.axis_index("xc")
    outer = lax.axis_size("zl")
    band = lax.axis_index("zl")
    place = member.astype(jnp.float32)
    inner_terms = cube_coefficients(inner, member)
    outer_terms = [inner * term for term in cube_coefficients(outer, band)]
    unit_terms = [place, inner - 1 - place, jnp.float32(1)]
    terms = jnp.stack(inner_terms + outer_terms + unit_terms)
    factors = jnp.exp(-decay_step[None] * terms[:, None, None])
    inner_rounds = cube_weights(factors, inner, member)
    outer_rounds = cube_weights(factors[len(inner_terms) :], outer, band)
    near, group, (rates, weights) = cube_scan(
        jnp.stack([end_state, start_state]), inner_rounds, "xc", inner, (rates, weights)
    )
    far, _, _ = cube_scan(group, outer_rounds, "zl", outer, ())
    entering = near[0] + factors[-3] * far[0]
    leaving = near[1] + factors[-2] * far[1]

    centred = jnp.arange(block_len).astype(jnp.float32) - block_len // 2
    falling = weights[:, None, :] * jnp.exp(-centred[None, :, None] * rates[:, None, :])
    rising = jnp.exp(centred[None, None, :] * rates[:, :, None])
    toeplitz = jnp.einsum("gtm,gms->gts", falling, rising, precision=precise)
    lower = jnp.arange(block_len)[:, None] >= jnp.arange(block_len)[None, :]
    toeplitz = jnp.where(lower[None], toeplitz, 0.0)
    local_conv = split_dot("gts,sgc->tgc", toeplitz, signal).reshape(block_len, channels)
    local_grad = split_dot("gts,tgc->sgc", toeplitz, cotangent).reshape(block_len, channels)
    lead_fwd = (weights[:, :, None] * powers[:, :, 1:]).reshape(group_count * order, block_len)
    lead_bwd = (weights[:, :, None] * powers[:, :, block_len:0:-1]).reshape(
        group_count * order, block_len
    )
    carried_conv = jnp.einsum("kt,kc->tc", lead_fwd, spread(entering), precision=precise)
    carried_grad = jnp.einsum("ks,kc->sc", lead_bwd, spread(leaving), precision=precise)
    conv_out = rounded(local_conv + carried_conv)
    grad_prod = rounded(local_grad + carried_grad)

    q_next = rounded(short_causal(rim_rows[0], after[0], short_filter[0]))
    k_next = rounded(short_causal(rim_rows[1], after[1], short_filter[1]))
    v_next = rounded(short_causal(rim_rows[2], after[2], short_filter[2]))
    p_next = rounded(k_next.astype(jnp.float32) * v_next.astype(jnp.float32))
    gc_next = rounded(after[3].astype(jnp.float32) * q_next.astype(jnp.float32))
    rate_rows = decay_step / block_len
    weight_rows = jnp.repeat(weights.T, GROUP, axis=1)
    lag_terms = jnp.concatenate([-jnp.arange(SHORT), jnp.arange(SHORT)]).astype(jnp.float32)
    lag_powers = jnp.exp(rate_rows[None] * lag_terms[:, None, None])
    falling_taps = (weight_rows[None] * lag_powers[:SHORT]).sum(1)
    rising_taps = (weight_rows[None] * lag_powers[SHORT:]).sum(1)
    rising_taps = jnp.where(jnp.arange(SHORT)[:, None] > 0, rising_taps, 0.0)
    through = factors[-1] * entering + end_state
    none_before = jnp.zeros((edge, channels), jnp.float32)
    next_conv = rounded(
        short_causal(none_before, p_next, falling_taps)
        + ((weight_rows * through)[None] * lag_powers[1:SHORT]).sum(1)
    )
    next_grad = rounded(
        ((weight_rows * leaving)[None] * lag_powers[SHORT : SHORT + edge]).sum(1)
        - short_causal(none_before, gc_next, rising_taps)
    )
    next_rows = (
        rounded(after[3].astype(jnp.float32) * next_conv.astype(jnp.float32)),
        rounded(next_grad.astype(jnp.float32) * v_next.astype(jnp.float32)),
        rounded(next_grad.astype(jnp.float32) * k_next.astype(jnp.float32)),
    )

    mixer_out = (q_short.astype(jnp.float32) * conv_out.astype(jnp.float32)).astype(jnp.bfloat16)
    grad_qshort = rounded(grad_out.astype(jnp.float32) * conv_out.astype(jnp.float32))
    grad_kshort = rounded(grad_prod.astype(jnp.float32) * v_short.astype(jnp.float32))
    grad_vshort = rounded(grad_prod.astype(jnp.float32) * k_short.astype(jnp.float32))
    grad_query = short_reverse(grad_qshort, next_rows[0], short_filter[0]).astype(jnp.bfloat16)
    grad_key = short_reverse(grad_kshort, next_rows[1], short_filter[1]).astype(jnp.bfloat16)
    grad_value = short_reverse(grad_vshort, next_rows[2], short_filter[2]).astype(jnp.bfloat16)
    return (mixer_out, grad_query, grad_key, grad_value)


def solution(mesh):
    ctx_count = mesh.shape["ctx"]
    inner = math.gcd(INNER, ctx_count)
    grid = Mesh(
        mesh.devices.reshape(ctx_count // inner, inner, mesh.shape["tp"]), ("zl", "xc", "tp")
    )
    rows = P(("zl", "xc"), "tp")
    return jax.shard_map(
        lambda *arrays: shards(inner, *arrays),
        mesh=grid,
        in_specs=(rows, rows, rows, P(None, None, "tp"), P("tp", None), P("tp", None), rows),
        out_specs=(rows, rows, rows, rows),
        check_vma=False,
    )
```

```python
import math

import jax
import jax.numpy as jnp
from jax import lax
from jax.sharding import Mesh, PartitionSpec as P

GROUP = 16
SHORT = 7
INNER = 8


precise = lax.Precision.HIGHEST


def from_behind(value, axis, steps):
    count = lax.axis_size(axis)
    leading, last = (max(0, -steps), min(count, count - steps))
    return lax.ppermute(value, axis, [(source, source + steps) for source in range(leading, last)])


def rounded(values):
    return lax.optimization_barrier(values.astype(jnp.bfloat16))


def short_causal(prior_rows, inputs, filter_taps):
    length = inputs.shape[0]
    padded = jnp.concatenate([prior_rows.astype(jnp.float32), inputs.astype(jnp.float32)], axis=0)
    summed = jnp.zeros(inputs.shape, jnp.float32)
    for offset in range(SHORT):
        summed = (
            summed + filter_taps[offset] * padded[SHORT - 1 - offset : SHORT - 1 - offset + length]
        )
    return summed


def short_reverse(grad_rows, next_rows, filter_taps):
    length = grad_rows.shape[0]
    padded = jnp.concatenate([grad_rows.astype(jnp.float32), next_rows.astype(jnp.float32)], axis=0)
    summed = jnp.zeros(grad_rows.shape, jnp.float32)
    for offset in range(SHORT):
        summed = summed + filter_taps[offset] * padded[offset : offset + length]
    return summed


def split_dot(spec, table, values):
    high = lax.reduce_precision(table, exponent_bits=8, mantissa_bits=7)
    low = (table - high).astype(jnp.bfloat16)
    lhs = jnp.einsum(spec, high.astype(jnp.bfloat16), values, preferred_element_type=jnp.float32)
    return lhs + jnp.einsum(spec, low, values, preferred_element_type=jnp.float32)


def cube_coefficients(size, index):
    terms = []
    shift = 1
    while shift < size:
        offset = (index % shift).astype(jnp.float32)
        terms += [jnp.float32(shift), offset, shift - 1 - offset]
        shift *= 2
    return terms


def cube_weights(factors, size, index):
    rounds = []
    shift = 1
    step = 0
    while shift < size:
        upper = (index & shift) != 0
        span, lead, trail = factors[step], factors[step + 1], factors[step + 2]
        one = jnp.ones_like(span)
        zero = jnp.zeros_like(span)
        keep = jnp.stack([jnp.where(upper, one, span), jnp.where(upper, span, one)])
        take = jnp.stack([jnp.where(upper, span, one), jnp.where(upper, one, span)])
        add = jnp.stack([jnp.where(upper, lead, zero), jnp.where(upper, zero, trail)])
        rounds.append((keep, take, add))
        shift *= 2
        step += 3
    return rounds


def cube_scan(window, rounds, axis, size, held):
    entering = jnp.zeros_like(window)
    shift = 1
    for keep, take, add in rounds:
        arrived = lax.ppermute(window, axis, [(source, source ^ shift) for source in range(size)])
        if shift == 1:
            held, arrived = lax.optimization_barrier((held, arrived))
        entering = entering + add * arrived
        window = keep * window + take * arrived
        shift *= 2
    return entering, window, held


def shards(inner, u_query, u_key, u_value, short_filter, decay_rate, residue, grad_out):
    block_len, channels = u_query.shape
    group_count = channels // GROUP
    rim_rows = jnp.stack(
        [
            u_query[block_len - SHORT + 1 :],
            u_key[block_len - SHORT + 1 :],
            u_value[block_len - SHORT + 1 :],
        ]
    )
    before = from_behind(rim_rows, ("zl", "xc"), 1)
    q_short = rounded(short_causal(before[0], u_query, short_filter[0]))
    k_short = rounded(short_causal(before[1], u_key, short_filter[1]))
    v_short = rounded(short_causal(before[2], u_value, short_filter[2]))
    product = rounded(k_short.astype(jnp.float32) * v_short.astype(jnp.float32))
    grad_conv = rounded(grad_out.astype(jnp.float32) * q_short.astype(jnp.float32))

    rates = decay_rate
    weights = residue * jnp.sqrt(-jnp.expm1(-2.0 * rates))
    lags = jnp.arange(block_len + 1).astype(jnp.float32)
    powers = jnp.exp(-rates[:, :, None] * lags)

    signal = product.reshape(block_len, group_count, GROUP)
    cotangent = grad_conv.reshape(block_len, group_count, GROUP)
    order = rates.shape[1]
    owner = (jnp.arange(channels) // GROUP)[None, :] == jnp.arange(group_count)[:, None]
    owner = owner.astype(jnp.float32)

    def own_block(full):
        return (full.reshape(group_count, order, channels) * owner[:, None, :]).sum(0)

    def spread(state):
        return (state[None] * owner[:, None, :]).reshape(group_count * order, channels)

    end_rows = powers[:, :, block_len - 1 :: -1].reshape(group_count * order, block_len)
    start_rows = powers[:, :, :block_len].reshape(group_count * order, block_len)
    end_state = own_block(split_dot("ks,sc->kc", end_rows, product))
    start_state = own_block(split_dot("ks,sc->kc", start_rows, grad_conv))
    decay_step = jnp.repeat(rates.T, GROUP, axis=1) * block_len
    member = lax.axis_index("xc")
    outer = lax.axis_size("zl")
    band = lax.axis_index("zl")
    place = member.astype(jnp.float32)
    inner_terms = cube_coefficients(inner, member)
    outer_terms = [inner * term for term in cube_coefficients(outer, band)]
    unit_terms = [place, inner - 1 - place, jnp.float32(1), jnp.float32(-1)]
    terms = jnp.stack(inner_terms + outer_terms + unit_terms)
    factors = jnp.exp(-decay_step[None] * terms[:, None, None])
    inner_rounds = cube_weights(factors, inner, member)
    outer_rounds = cube_weights(factors[len(inner_terms) :], outer, band)
    near, group, (rates, weights) = cube_scan(
        jnp.stack([end_state, start_state]), inner_rounds, "xc", inner, (rates, weights)
    )

    centred = jnp.arange(block_len).astype(jnp.float32) - block_len // 2
    falling = weights[:, None, :] * jnp.exp(-centred[None, :, None] * rates[:, None, :])
    rising = jnp.exp(centred[None, None, :] * rates[:, :, None])
    toeplitz = jnp.einsum("gtm,gms->gts", falling, rising, precision=precise)
    lower = jnp.arange(block_len)[:, None] >= jnp.arange(block_len)[None, :]
    toeplitz = jnp.where(lower[None], toeplitz, 0.0)
    local_conv = split_dot("gts,sgc->tgc", toeplitz, signal).reshape(block_len, channels)
    local_grad = split_dot("gts,tgc->sgc", toeplitz, cotangent).reshape(block_len, channels)
    edge = SHORT - 1
    slab = 8
    pieces = [local_conv, local_grad, grad_out, k_short, v_short]
    ahead = jnp.concatenate(
        [piece[:slab].astype(jnp.float32) for piece in pieces] + [start_state]
    )
    ahead = from_behind(ahead, ("zl", "xc"), -1)
    far, _, ahead = cube_scan(group, outer_rounds, "zl", outer, ahead)
    entering = near[0] + factors[-4] * far[0]
    leaving = near[1] + factors[-3] * far[1]
    next_local_conv, next_local_grad, next_grad_out, next_k, next_v = (
        ahead[slab * piece : slab * piece + edge] for piece in range(len(pieces))
    )
    next_start = ahead[slab * len(pieces) :]
    lead_fwd = (weights[:, :, None] * powers[:, :, 1:]).reshape(group_count * order, block_len)
    lead_bwd = (weights[:, :, None] * powers[:, :, block_len:0:-1]).reshape(
        group_count * order, block_len
    )
    carried_conv = jnp.einsum("kt,kc->tc", lead_fwd, spread(entering), precision=precise)
    carried_grad = jnp.einsum("ks,kc->sc", lead_bwd, spread(leaving), precision=precise)
    conv_out = rounded(local_conv + carried_conv)
    grad_prod = rounded(local_grad + carried_grad)

    through = factors[-2] * entering + end_state
    beyond = (leaving - next_start) * factors[-1]
    next_conv = rounded(
        next_local_conv
        + jnp.einsum("kt,kc->tc", lead_fwd[:, :edge], spread(through), precision=precise)
    )
    next_grad = rounded(
        next_local_grad
        + jnp.einsum("ks,kc->sc", lead_bwd[:, :edge], spread(beyond), precision=precise)
    )
    next_rows = (
        rounded(next_grad_out.astype(jnp.float32) * next_conv.astype(jnp.float32)),
        rounded(next_grad.astype(jnp.float32) * next_v.astype(jnp.float32)),
        rounded(next_grad.astype(jnp.float32) * next_k.astype(jnp.float32)),
    )

    mixer_out = (q_short.astype(jnp.float32) * conv_out.astype(jnp.float32)).astype(jnp.bfloat16)
    grad_qshort = rounded(grad_out.astype(jnp.float32) * conv_out.astype(jnp.float32))
    grad_kshort = rounded(grad_prod.astype(jnp.float32) * v_short.astype(jnp.float32))
    grad_vshort = rounded(grad_prod.astype(jnp.float32) * k_short.astype(jnp.float32))
    grad_query = short_reverse(grad_qshort, next_rows[0], short_filter[0]).astype(jnp.bfloat16)
    grad_key = short_reverse(grad_kshort, next_rows[1], short_filter[1]).astype(jnp.bfloat16)
    grad_value = short_reverse(grad_vshort, next_rows[2], short_filter[2]).astype(jnp.bfloat16)
    return (mixer_out, grad_query, grad_key, grad_value)


def solution(mesh):
    ctx_count = mesh.shape["ctx"]
    inner = math.gcd(INNER, ctx_count)
    grid = Mesh(
        mesh.devices.reshape(ctx_count // inner, inner, mesh.shape["tp"]), ("zl", "xc", "tp")
    )
    rows = P(("zl", "xc"), "tp")
    return jax.shard_map(
        lambda *arrays: shards(inner, *arrays),
        mesh=grid,
        in_specs=(rows, rows, rows, P(None, None, "tp"), P("tp", None), P("tp", None), rows),
        out_specs=(rows, rows, rows, rows),
        check_vma=False,
    )
```

```python
import math

import jax
import jax.numpy as jnp
from jax import lax
from jax.sharding import Mesh, PartitionSpec as P

GROUP = 16
SHORT = 7
INNER = 8


precise = lax.Precision.HIGHEST


def from_behind(value, axis, steps):
    count = lax.axis_size(axis)
    leading, last = (max(0, -steps), min(count, count - steps))
    return lax.ppermute(value, axis, [(source, source + steps) for source in range(leading, last)])


def rounded(values):
    return lax.optimization_barrier(values.astype(jnp.bfloat16))


def short_causal(prior_rows, inputs, filter_taps):
    length = inputs.shape[0]
    padded = jnp.concatenate([prior_rows.astype(jnp.float32), inputs.astype(jnp.float32)], axis=0)
    summed = jnp.zeros(inputs.shape, jnp.float32)
    for offset in range(SHORT):
        summed = (
            summed + filter_taps[offset] * padded[SHORT - 1 - offset : SHORT - 1 - offset + length]
        )
    return summed


def short_reverse(grad_rows, next_rows, filter_taps):
    length = grad_rows.shape[0]
    padded = jnp.concatenate([grad_rows.astype(jnp.float32), next_rows.astype(jnp.float32)], axis=0)
    summed = jnp.zeros(grad_rows.shape, jnp.float32)
    for offset in range(SHORT):
        summed = summed + filter_taps[offset] * padded[offset : offset + length]
    return summed


def split_dot(spec, table, values):
    high = lax.reduce_precision(table, exponent_bits=8, mantissa_bits=7)
    low = (table - high).astype(jnp.bfloat16)
    lhs = jnp.einsum(spec, high.astype(jnp.bfloat16), values, preferred_element_type=jnp.float32)
    return lhs + jnp.einsum(spec, low, values, preferred_element_type=jnp.float32)


def cube_coefficients(size, index):
    terms = []
    shift = 1
    while shift < size:
        offset = (index % shift).astype(jnp.float32)
        terms += [jnp.float32(shift), offset, shift - 1 - offset]
        shift *= 2
    return terms


def cube_weights(factors, size, index):
    rounds = []
    shift = 1
    step = 0
    while shift < size:
        upper = (index & shift) != 0
        span, lead, trail = factors[step], factors[step + 1], factors[step + 2]
        one = jnp.ones_like(span)
        zero = jnp.zeros_like(span)
        keep = jnp.stack([jnp.where(upper, one, span), jnp.where(upper, span, one)])
        take = jnp.stack([jnp.where(upper, span, one), jnp.where(upper, one, span)])
        add = jnp.stack([jnp.where(upper, lead, zero), jnp.where(upper, zero, trail)])
        rounds.append((keep, take, add))
        shift *= 2
        step += 3
    return rounds


def cube_scan(window, rounds, axis, size, held):
    entering = jnp.zeros_like(window)
    shift = 1
    for keep, take, add in rounds:
        arrived = lax.ppermute(window, axis, [(source, source ^ shift) for source in range(size)])
        if shift == 1:
            held, arrived = lax.optimization_barrier((held, arrived))
        entering = entering + add * arrived
        window = keep * window + take * arrived
        shift *= 2
    return entering, window, held


def shards(inner, u_query, u_key, u_value, short_filter, decay_rate, residue, grad_out):
    block_len, channels = u_query.shape
    group_count = channels // GROUP
    rim_rows = jnp.stack(
        [
            u_query[block_len - SHORT + 1 :],
            u_key[block_len - SHORT + 1 :],
            u_value[block_len - SHORT + 1 :],
        ]
    )
    before = from_behind(rim_rows, ("zl", "xc"), 1)
    q_short = rounded(short_causal(before[0], u_query, short_filter[0]))
    k_short = rounded(short_causal(before[1], u_key, short_filter[1]))
    v_short = rounded(short_causal(before[2], u_value, short_filter[2]))
    product = rounded(k_short.astype(jnp.float32) * v_short.astype(jnp.float32))
    grad_conv = rounded(grad_out.astype(jnp.float32) * q_short.astype(jnp.float32))

    rates = decay_rate
    weights = residue * jnp.sqrt(-jnp.expm1(-2.0 * rates))
    lags = jnp.arange(block_len + 1).astype(jnp.float32)
    powers = jnp.exp(-rates[:, :, None] * lags)

    signal = product.reshape(block_len, group_count, GROUP)
    cotangent = grad_conv.reshape(block_len, group_count, GROUP)
    order = rates.shape[1]
    owner = (jnp.arange(channels) // GROUP)[None, :] == jnp.arange(group_count)[:, None]
    owner = owner.astype(jnp.float32)

    def own_block(full):
        return (full.reshape(group_count, order, channels) * owner[:, None, :]).sum(0)

    def spread(state):
        return (state[None] * owner[:, None, :]).reshape(group_count * order, channels)

    end_rows = powers[:, :, block_len - 1 :: -1].reshape(group_count * order, block_len)
    start_rows = powers[:, :, :block_len].reshape(group_count * order, block_len)
    end_state = own_block(split_dot("ks,sc->kc", end_rows, product))
    start_state = own_block(split_dot("ks,sc->kc", start_rows, grad_conv))
    decay_step = jnp.repeat(rates.T, GROUP, axis=1) * block_len
    member = lax.axis_index("xc")
    outer = lax.axis_size("zl")
    band = lax.axis_index("zl")
    place = member.astype(jnp.float32)
    inner_terms = cube_coefficients(inner, member)
    outer_terms = [inner * term for term in cube_coefficients(outer, band)]
    unit_terms = [place, inner - 1 - place, jnp.float32(1), jnp.float32(-1)]
    terms = jnp.stack(inner_terms + outer_terms + unit_terms)
    factors = jnp.exp(-decay_step[None] * terms[:, None, None])
    inner_rounds = cube_weights(factors, inner, member)
    outer_rounds = cube_weights(factors[len(inner_terms) :], outer, band)
    near, group, (rates, weights) = cube_scan(
        jnp.stack([end_state, start_state]), inner_rounds, "xc", inner, (rates, weights)
    )
    far, _, _ = cube_scan(group, outer_rounds, "zl", outer, ())
    entering = near[0] + factors[-4] * far[0]
    leaving = near[1] + factors[-3] * far[1]

    centred = jnp.arange(block_len).astype(jnp.float32) - block_len // 2
    falling = weights[:, None, :] * jnp.exp(-centred[None, :, None] * rates[:, None, :])
    rising = jnp.exp(centred[None, None, :] * rates[:, :, None])
    toeplitz = jnp.einsum("gtm,gms->gts", falling, rising, precision=precise)
    lower = jnp.arange(block_len)[:, None] >= jnp.arange(block_len)[None, :]
    toeplitz = jnp.where(lower[None], toeplitz, 0.0)
    local_conv = split_dot("gts,sgc->tgc", toeplitz, signal).reshape(block_len, channels)
    local_grad = split_dot("gts,tgc->sgc", toeplitz, cotangent).reshape(block_len, channels)
    lead_fwd = (weights[:, :, None] * powers[:, :, 1:]).reshape(group_count * order, block_len)
    lead_bwd = (weights[:, :, None] * powers[:, :, block_len:0:-1]).reshape(
        group_count * order, block_len
    )
    carried_conv = jnp.einsum("kt,kc->tc", lead_fwd, spread(entering), precision=precise)
    carried_grad = jnp.einsum("ks,kc->sc", lead_bwd, spread(leaving), precision=precise)
    conv_out = rounded(local_conv + carried_conv)
    grad_prod = rounded(local_grad + carried_grad)

    edge = SHORT - 1
    slab = 8
    pieces = [local_conv, local_grad, grad_out, k_short, v_short]
    ahead = jnp.concatenate(
        [piece[:slab].astype(jnp.float32) for piece in pieces] + [start_state]
    )
    ahead = from_behind(ahead, ("zl", "xc"), -1)
    through = factors[-2] * entering + end_state
    beyond = (leaving - ahead[slab * len(pieces) :]) * factors[-1]
    next_conv = rounded(
        ahead[:edge]
        + jnp.einsum("kt,kc->tc", lead_fwd[:, :edge], spread(through), precision=precise)
    )
    next_grad = rounded(
        ahead[slab : slab + edge]
        + jnp.einsum("ks,kc->sc", lead_bwd[:, :edge], spread(beyond), precision=precise)
    )
    next_rows = (
        rounded(ahead[2 * slab : 2 * slab + edge] * next_conv.astype(jnp.float32)),
        rounded(next_grad.astype(jnp.float32) * ahead[4 * slab : 4 * slab + edge]),
        rounded(next_grad.astype(jnp.float32) * ahead[3 * slab : 3 * slab + edge]),
    )

    mixer_out = (q_short.astype(jnp.float32) * conv_out.astype(jnp.float32)).astype(jnp.bfloat16)
    grad_qshort = rounded(grad_out.astype(jnp.float32) * conv_out.astype(jnp.float32))
    grad_kshort = rounded(grad_prod.astype(jnp.float32) * v_short.astype(jnp.float32))
    grad_vshort = rounded(grad_prod.astype(jnp.float32) * k_short.astype(jnp.float32))
    grad_query = short_reverse(grad_qshort, next_rows[0], short_filter[0]).astype(jnp.bfloat16)
    grad_key = short_reverse(grad_kshort, next_rows[1], short_filter[1]).astype(jnp.bfloat16)
    grad_value = short_reverse(grad_vshort, next_rows[2], short_filter[2]).astype(jnp.bfloat16)
    return (mixer_out, grad_query, grad_key, grad_value)


def solution(mesh):
    ctx_count = mesh.shape["ctx"]
    inner = math.gcd(INNER, ctx_count)
    grid = Mesh(
        mesh.devices.reshape(ctx_count // inner, inner, mesh.shape["tp"]), ("zl", "xc", "tp")
    )
    rows = P(("zl", "xc"), "tp")
    return jax.shard_map(
        lambda *arrays: shards(inner, *arrays),
        mesh=grid,
        in_specs=(rows, rows, rows, P(None, None, "tp"), P("tp", None), P("tp", None), rows),
        out_specs=(rows, rows, rows, rows),
        check_vma=False,
    )
```

```python
import math

import jax
import jax.numpy as jnp
from jax import lax
from jax.sharding import Mesh, PartitionSpec as P

GROUP = 16
SHORT = 7
INNER = 8


precise = lax.Precision.HIGHEST


def from_behind(value, axis, steps):
    count = lax.axis_size(axis)
    leading, last = (max(0, -steps), min(count, count - steps))
    return lax.ppermute(value, axis, [(source, source + steps) for source in range(leading, last)])


def rounded(values):
    return lax.optimization_barrier(values.astype(jnp.bfloat16))


def short_causal(prior_rows, inputs, filter_taps):
    length = inputs.shape[0]
    padded = jnp.concatenate([prior_rows.astype(jnp.float32), inputs.astype(jnp.float32)], axis=0)
    summed = jnp.zeros(inputs.shape, jnp.float32)
    for offset in range(SHORT):
        summed = (
            summed + filter_taps[offset] * padded[SHORT - 1 - offset : SHORT - 1 - offset + length]
        )
    return summed


def short_reverse(grad_rows, next_rows, filter_taps):
    length = grad_rows.shape[0]
    padded = jnp.concatenate([grad_rows.astype(jnp.float32), next_rows.astype(jnp.float32)], axis=0)
    summed = jnp.zeros(grad_rows.shape, jnp.float32)
    for offset in range(SHORT):
        summed = summed + filter_taps[offset] * padded[offset : offset + length]
    return summed


def split_dot(spec, table, values):
    high = lax.reduce_precision(table, exponent_bits=8, mantissa_bits=7)
    low = (table - high).astype(jnp.bfloat16)
    lhs = jnp.einsum(spec, high.astype(jnp.bfloat16), values, preferred_element_type=jnp.float32)
    return lhs + jnp.einsum(spec, low, values, preferred_element_type=jnp.float32)


def cube_coefficients(size, index):
    terms = []
    shift = 1
    while shift < size:
        offset = (index % shift).astype(jnp.float32)
        terms += [jnp.float32(shift), offset, shift - 1 - offset]
        shift *= 2
    return terms


def cube_weights(factors, size, index):
    rounds = []
    shift = 1
    step = 0
    while shift < size:
        upper = (index & shift) != 0
        span, lead, trail = factors[step], factors[step + 1], factors[step + 2]
        one = jnp.ones_like(span)
        zero = jnp.zeros_like(span)
        keep = jnp.stack([jnp.where(upper, one, span), jnp.where(upper, span, one)])
        take = jnp.stack([jnp.where(upper, span, one), jnp.where(upper, one, span)])
        add = jnp.stack([jnp.where(upper, lead, zero), jnp.where(upper, zero, trail)])
        rounds.append((keep, take, add))
        shift *= 2
        step += 3
    return rounds


def cube_scan(window, rounds, axis, size, held):
    entering = jnp.zeros_like(window)
    shift = 1
    for keep, take, add in rounds:
        arrived = lax.ppermute(window, axis, [(source, source ^ shift) for source in range(size)])
        if shift == 1:
            held, arrived = lax.optimization_barrier((held, arrived))
        entering = entering + add * arrived
        window = keep * window + take * arrived
        shift *= 2
    return entering, window, held


def shards(inner, u_query, u_key, u_value, short_filter, decay_rate, residue, grad_out):
    block_len, channels = u_query.shape
    group_count = channels // GROUP
    rim_rows = jnp.stack(
        [
            u_query[block_len - SHORT + 1 :],
            u_key[block_len - SHORT + 1 :],
            u_value[block_len - SHORT + 1 :],
        ]
    )
    before = from_behind(rim_rows, ("zl", "xc"), 1)
    q_short = rounded(short_causal(before[0], u_query, short_filter[0]))
    k_short = rounded(short_causal(before[1], u_key, short_filter[1]))
    v_short = rounded(short_causal(before[2], u_value, short_filter[2]))
    product = rounded(k_short.astype(jnp.float32) * v_short.astype(jnp.float32))
    grad_conv = rounded(grad_out.astype(jnp.float32) * q_short.astype(jnp.float32))

    rates = decay_rate
    weights = residue * jnp.sqrt(-jnp.expm1(-2.0 * rates))
    lags = jnp.arange(block_len + 1).astype(jnp.float32)
    powers = jnp.exp(-rates[:, :, None] * lags)

    signal = product.reshape(block_len, group_count, GROUP)
    cotangent = grad_conv.reshape(block_len, group_count, GROUP)
    order = rates.shape[1]
    owner = (jnp.arange(channels) // GROUP)[None, :] == jnp.arange(group_count)[:, None]
    owner = owner.astype(jnp.float32)

    def own_block(full):
        return (full.reshape(group_count, order, channels) * owner[:, None, :]).sum(0)

    def spread(state):
        return (state[None] * owner[:, None, :]).reshape(group_count * order, channels)

    end_rows = powers[:, :, block_len - 1 :: -1].reshape(group_count * order, block_len)
    start_rows = powers[:, :, :block_len].reshape(group_count * order, block_len)
    end_state = own_block(split_dot("ks,sc->kc", end_rows, product))
    start_state = own_block(split_dot("ks,sc->kc", start_rows, grad_conv))
    decay_step = jnp.repeat(rates.T, GROUP, axis=1) * block_len
    member = lax.axis_index("xc")
    outer = lax.axis_size("zl")
    band = lax.axis_index("zl")
    place = member.astype(jnp.float32)
    inner_terms = cube_coefficients(inner, member)
    outer_terms = [inner * term for term in cube_coefficients(outer, band)]
    unit_terms = [place, inner - 1 - place, jnp.float32(1)]
    terms = jnp.stack(inner_terms + outer_terms + unit_terms)
    factors = jnp.exp(-decay_step[None] * terms[:, None, None])
    inner_rounds = cube_weights(factors, inner, member)
    outer_rounds = cube_weights(factors[len(inner_terms) :], outer, band)
    near, group, (rates, weights) = cube_scan(
        jnp.stack([end_state, start_state]), inner_rounds, "xc", inner, (rates, weights)
    )
    edge = SHORT - 1
    head_rows = jnp.stack([q_short[:edge], k_short[:edge], v_short[:edge], grad_out[:edge]])
    after = from_behind(head_rows, ("zl", "xc"), -1)
    far, _, after = cube_scan(group, outer_rounds, "zl", outer, after)
    entering = near[0] + factors[-3] * far[0]
    leaving = near[1] + factors[-2] * far[1]

    centred = jnp.arange(block_len).astype(jnp.float32) - block_len // 2
    falling = weights[:, None, :] * jnp.exp(-centred[None, :, None] * rates[:, None, :])
    rising = jnp.exp(centred[None, None, :] * rates[:, :, None])
    toeplitz = jnp.einsum("gtm,gms->gts", falling, rising, precision=precise)
    lower = jnp.arange(block_len)[:, None] >= jnp.arange(block_len)[None, :]
    toeplitz = jnp.where(lower[None], toeplitz, 0.0)
    local_conv = split_dot("gts,sgc->tgc", toeplitz, signal).reshape(block_len, channels)
    local_grad = split_dot("gts,tgc->sgc", toeplitz, cotangent).reshape(block_len, channels)
    lead_fwd = (weights[:, :, None] * powers[:, :, 1:]).reshape(group_count * order, block_len)
    lead_bwd = (weights[:, :, None] * powers[:, :, block_len:0:-1]).reshape(
        group_count * order, block_len
    )
    carried_conv = jnp.einsum("kt,kc->tc", lead_fwd, spread(entering), precision=precise)
    carried_grad = jnp.einsum("ks,kc->sc", lead_bwd, spread(leaving), precision=precise)
    conv_out = rounded(local_conv + carried_conv)
    grad_prod = rounded(local_grad + carried_grad)

    q_next, k_next, v_next, go_next = (after[row].astype(jnp.float32) for row in range(4))
    p_next = rounded(k_next * v_next)
    gc_next = rounded(go_next * q_next)
    rate_rows = decay_step / block_len
    weight_rows = jnp.repeat(weights.T, GROUP, axis=1)
    lag_terms = jnp.concatenate([-jnp.arange(SHORT), jnp.arange(SHORT)]).astype(jnp.float32)
    lag_powers = jnp.exp(rate_rows[None] * lag_terms[:, None, None])
    falling_taps = (weight_rows[None] * lag_powers[:SHORT]).sum(1)
    rising_taps = (weight_rows[None] * lag_powers[SHORT:]).sum(1)
    rising_taps = jnp.where(jnp.arange(SHORT)[:, None] > 0, rising_taps, 0.0)
    through = factors[-1] * entering + end_state
    none_before = jnp.zeros((edge, channels), jnp.float32)
    next_conv = rounded(
        short_causal(none_before, p_next, falling_taps)
        + ((weight_rows * through)[None] * lag_powers[1:SHORT]).sum(1)
    )
    next_grad = rounded(
        ((weight_rows * leaving)[None] * lag_powers[SHORT : SHORT + edge]).sum(1)
        - short_causal(none_before, gc_next, rising_taps)
    )
    next_rows = (
        rounded(go_next * next_conv.astype(jnp.float32)),
        rounded(next_grad.astype(jnp.float32) * v_next),
        rounded(next_grad.astype(jnp.float32) * k_next),
    )

    mixer_out = (q_short.astype(jnp.float32) * conv_out.astype(jnp.float32)).astype(jnp.bfloat16)
    grad_qshort = rounded(grad_out.astype(jnp.float32) * conv_out.astype(jnp.float32))
    grad_kshort = rounded(grad_prod.astype(jnp.float32) * v_short.astype(jnp.float32))
    grad_vshort = rounded(grad_prod.astype(jnp.float32) * k_short.astype(jnp.float32))
    grad_query = short_reverse(grad_qshort, next_rows[0], short_filter[0]).astype(jnp.bfloat16)
    grad_key = short_reverse(grad_kshort, next_rows[1], short_filter[1]).astype(jnp.bfloat16)
    grad_value = short_reverse(grad_vshort, next_rows[2], short_filter[2]).astype(jnp.bfloat16)
    return (mixer_out, grad_query, grad_key, grad_value)


def solution(mesh):
    ctx_count = mesh.shape["ctx"]
    inner = math.gcd(INNER, ctx_count)
    grid = Mesh(
        mesh.devices.reshape(ctx_count // inner, inner, mesh.shape["tp"]), ("zl", "xc", "tp")
    )
    rows = P(("zl", "xc"), "tp")
    return jax.shard_map(
        lambda *arrays: shards(inner, *arrays),
        mesh=grid,
        in_specs=(rows, rows, rows, P(None, None, "tp"), P("tp", None), P("tp", None), rows),
        out_specs=(rows, rows, rows, rows),
        check_vma=False,
    )
```

```python
import math

import jax
import jax.numpy as jnp
from jax import lax
from jax.sharding import Mesh, PartitionSpec as P

GROUP = 16
SHORT = 7
INNER = 8


precise = lax.Precision.HIGHEST


def from_behind(value, axis, steps):
    count = lax.axis_size(axis)
    leading, last = (max(0, -steps), min(count, count - steps))
    return lax.ppermute(value, axis, [(source, source + steps) for source in range(leading, last)])


def rounded(values):
    return lax.optimization_barrier(values.astype(jnp.bfloat16))


def short_causal(prior_rows, inputs, filter_taps):
    length = inputs.shape[0]
    padded = jnp.concatenate([prior_rows.astype(jnp.float32), inputs.astype(jnp.float32)], axis=0)
    summed = jnp.zeros(inputs.shape, jnp.float32)
    for offset in range(SHORT):
        summed = (
            summed + filter_taps[offset] * padded[SHORT - 1 - offset : SHORT - 1 - offset + length]
        )
    return summed


def short_reverse(grad_rows, next_rows, filter_taps):
    length = grad_rows.shape[0]
    padded = jnp.concatenate([grad_rows.astype(jnp.float32), next_rows.astype(jnp.float32)], axis=0)
    summed = jnp.zeros(grad_rows.shape, jnp.float32)
    for offset in range(SHORT):
        summed = summed + filter_taps[offset] * padded[offset : offset + length]
    return summed


def split_dot(spec, table, values):
    high = lax.reduce_precision(table, exponent_bits=8, mantissa_bits=7)
    low = (table - high).astype(jnp.bfloat16)
    lhs = jnp.einsum(spec, high.astype(jnp.bfloat16), values, preferred_element_type=jnp.float32)
    return lhs + jnp.einsum(spec, low, values, preferred_element_type=jnp.float32)


def cube_coefficients(size, index):
    terms = []
    shift = 1
    while shift < size:
        offset = (index % shift).astype(jnp.float32)
        terms += [jnp.float32(shift), offset, shift - 1 - offset]
        shift *= 2
    return terms


def cube_weights(factors, size, index):
    rounds = []
    shift = 1
    step = 0
    while shift < size:
        upper = (index & shift) != 0
        span, lead, trail = factors[step], factors[step + 1], factors[step + 2]
        one = jnp.ones_like(span)
        zero = jnp.zeros_like(span)
        keep = jnp.stack([jnp.where(upper, one, span), jnp.where(upper, span, one)])
        take = jnp.stack([jnp.where(upper, span, one), jnp.where(upper, one, span)])
        add = jnp.stack([jnp.where(upper, lead, zero), jnp.where(upper, zero, trail)])
        rounds.append((keep, take, add))
        shift *= 2
        step += 3
    return rounds


def cube_scan(window, rounds, axis, size, held, hold_at=1):
    entering = jnp.zeros_like(window)
    shift = 1
    for keep, take, add in rounds:
        arrived = lax.ppermute(window, axis, [(source, source ^ shift) for source in range(size)])
        if shift == hold_at:
            held, arrived = lax.optimization_barrier((held, arrived))
        entering = entering + add * arrived
        window = keep * window + take * arrived
        shift *= 2
    return entering, window, held


def shards(inner, u_query, u_key, u_value, short_filter, decay_rate, residue, grad_out):
    block_len, channels = u_query.shape
    group_count = channels // GROUP
    rim_rows = jnp.stack(
        [
            u_query[block_len - SHORT + 1 :],
            u_key[block_len - SHORT + 1 :],
            u_value[block_len - SHORT + 1 :],
        ]
    )
    before = from_behind(rim_rows, ("zl", "xc"), 1)
    q_short = rounded(short_causal(before[0], u_query, short_filter[0]))
    k_short = rounded(short_causal(before[1], u_key, short_filter[1]))
    v_short = rounded(short_causal(before[2], u_value, short_filter[2]))
    product = rounded(k_short.astype(jnp.float32) * v_short.astype(jnp.float32))
    grad_conv = rounded(grad_out.astype(jnp.float32) * q_short.astype(jnp.float32))

    rates = decay_rate
    weights = residue * jnp.sqrt(-jnp.expm1(-2.0 * rates))
    lags = jnp.arange(block_len + 1).astype(jnp.float32)
    powers = jnp.exp(-rates[:, :, None] * lags)

    signal = product.reshape(block_len, group_count, GROUP)
    cotangent = grad_conv.reshape(block_len, group_count, GROUP)
    order = rates.shape[1]
    owner = (jnp.arange(channels) // GROUP)[None, :] == jnp.arange(group_count)[:, None]
    owner = owner.astype(jnp.float32)

    def own_block(full):
        return (full.reshape(group_count, order, channels) * owner[:, None, :]).sum(0)

    def spread(state):
        return (state[None] * owner[:, None, :]).reshape(group_count * order, channels)

    end_rows = powers[:, :, block_len - 1 :: -1].reshape(group_count * order, block_len)
    start_rows = powers[:, :, :block_len].reshape(group_count * order, block_len)
    end_state = own_block(split_dot("ks,sc->kc", end_rows, product))
    start_state = own_block(split_dot("ks,sc->kc", start_rows, grad_conv))
    decay_step = jnp.repeat(rates.T, GROUP, axis=1) * block_len
    member = lax.axis_index("xc")
    outer = lax.axis_size("zl")
    band = lax.axis_index("zl")
    place = member.astype(jnp.float32)
    inner_terms = cube_coefficients(inner, member)
    outer_terms = [inner * term for term in cube_coefficients(outer, band)]
    unit_terms = [place, inner - 1 - place, jnp.float32(1)]
    terms = jnp.stack(inner_terms + outer_terms + unit_terms)
    factors = jnp.exp(-decay_step[None] * terms[:, None, None])
    inner_rounds = cube_weights(factors, inner, member)
    outer_rounds = cube_weights(factors[len(inner_terms) :], outer, band)
    near, group, (rates, weights) = cube_scan(
        jnp.stack([end_state, start_state]), inner_rounds, "xc", inner, (rates, weights), 2
    )
    edge = SHORT - 1
    head_rows = jnp.stack([q_short[:edge], k_short[:edge], v_short[:edge], grad_out[:edge]])
    after = from_behind(head_rows, ("zl", "xc"), -1)
    far, _, after = cube_scan(group, outer_rounds, "zl", outer, after)
    entering = near[0] + factors[-3] * far[0]
    leaving = near[1] + factors[-2] * far[1]

    centred = jnp.arange(block_len).astype(jnp.float32) - block_len // 2
    falling = weights[:, None, :] * jnp.exp(-centred[None, :, None] * rates[:, None, :])
    rising = jnp.exp(centred[None, None, :] * rates[:, :, None])
    toeplitz = jnp.einsum("gtm,gms->gts", falling, rising, precision=precise)
    lower = jnp.arange(block_len)[:, None] >= jnp.arange(block_len)[None, :]
    toeplitz = jnp.where(lower[None], toeplitz, 0.0)
    local_conv = split_dot("gts,sgc->tgc", toeplitz, signal).reshape(block_len, channels)
    local_grad = split_dot("gts,tgc->sgc", toeplitz, cotangent).reshape(block_len, channels)
    lead_fwd = (weights[:, :, None] * powers[:, :, 1:]).reshape(group_count * order, block_len)
    lead_bwd = (weights[:, :, None] * powers[:, :, block_len:0:-1]).reshape(
        group_count * order, block_len
    )
    carried_conv = jnp.einsum("kt,kc->tc", lead_fwd, spread(entering), precision=precise)
    carried_grad = jnp.einsum("ks,kc->sc", lead_bwd, spread(leaving), precision=precise)
    conv_out = rounded(local_conv + carried_conv)
    grad_prod = rounded(local_grad + carried_grad)

    q_next, k_next, v_next, go_next = (after[row].astype(jnp.float32) for row in range(4))
    p_next = rounded(k_next * v_next)
    gc_next = rounded(go_next * q_next)
    rate_rows = decay_step / block_len
    weight_rows = jnp.repeat(weights.T, GROUP, axis=1)
    lag_terms = jnp.concatenate([-jnp.arange(SHORT), jnp.arange(SHORT)]).astype(jnp.float32)
    lag_powers = jnp.exp(rate_rows[None] * lag_terms[:, None, None])
    falling_taps = (weight_rows[None] * lag_powers[:SHORT]).sum(1)
    rising_taps = (weight_rows[None] * lag_powers[SHORT:]).sum(1)
    rising_taps = jnp.where(jnp.arange(SHORT)[:, None] > 0, rising_taps, 0.0)
    through = factors[-1] * entering + end_state
    none_before = jnp.zeros((edge, channels), jnp.float32)
    next_conv = rounded(
        short_causal(none_before, p_next, falling_taps)
        + ((weight_rows * through)[None] * lag_powers[1:SHORT]).sum(1)
    )
    next_grad = rounded(
        ((weight_rows * leaving)[None] * lag_powers[SHORT : SHORT + edge]).sum(1)
        - short_causal(none_before, gc_next, rising_taps)
    )
    next_rows = (
        rounded(go_next * next_conv.astype(jnp.float32)),
        rounded(next_grad.astype(jnp.float32) * v_next),
        rounded(next_grad.astype(jnp.float32) * k_next),
    )

    mixer_out = (q_short.astype(jnp.float32) * conv_out.astype(jnp.float32)).astype(jnp.bfloat16)
    grad_qshort = rounded(grad_out.astype(jnp.float32) * conv_out.astype(jnp.float32))
    grad_kshort = rounded(grad_prod.astype(jnp.float32) * v_short.astype(jnp.float32))
    grad_vshort = rounded(grad_prod.astype(jnp.float32) * k_short.astype(jnp.float32))
    grad_query = short_reverse(grad_qshort, next_rows[0], short_filter[0]).astype(jnp.bfloat16)
    grad_key = short_reverse(grad_kshort, next_rows[1], short_filter[1]).astype(jnp.bfloat16)
    grad_value = short_reverse(grad_vshort, next_rows[2], short_filter[2]).astype(jnp.bfloat16)
    return (mixer_out, grad_query, grad_key, grad_value)


def solution(mesh):
    ctx_count = mesh.shape["ctx"]
    inner = math.gcd(INNER, ctx_count)
    grid = Mesh(
        mesh.devices.reshape(ctx_count // inner, inner, mesh.shape["tp"]), ("zl", "xc", "tp")
    )
    rows = P(("zl", "xc"), "tp")
    return jax.shard_map(
        lambda *arrays: shards(inner, *arrays),
        mesh=grid,
        in_specs=(rows, rows, rows, P(None, None, "tp"), P("tp", None), P("tp", None), rows),
        out_specs=(rows, rows, rows, rows),
        check_vma=False,
    )
```

```python
import math

import jax
import jax.numpy as jnp
from jax import lax
from jax.sharding import Mesh, PartitionSpec as P

GROUP = 16
SHORT = 7
INNER = 8


precise = lax.Precision.HIGHEST


def from_behind(value, axis, steps):
    count = lax.axis_size(axis)
    leading, last = (max(0, -steps), min(count, count - steps))
    return lax.ppermute(value, axis, [(source, source + steps) for source in range(leading, last)])


def rounded(values):
    return lax.optimization_barrier(values.astype(jnp.bfloat16))


def short_causal(prior_rows, inputs, filter_taps):
    length = inputs.shape[0]
    padded = jnp.concatenate([prior_rows.astype(jnp.float32), inputs.astype(jnp.float32)], axis=0)
    summed = jnp.zeros(inputs.shape, jnp.float32)
    for offset in range(SHORT):
        summed = (
            summed + filter_taps[offset] * padded[SHORT - 1 - offset : SHORT - 1 - offset + length]
        )
    return summed


def short_reverse(grad_rows, next_rows, filter_taps):
    length = grad_rows.shape[0]
    padded = jnp.concatenate([grad_rows.astype(jnp.float32), next_rows.astype(jnp.float32)], axis=0)
    summed = jnp.zeros(grad_rows.shape, jnp.float32)
    for offset in range(SHORT):
        summed = summed + filter_taps[offset] * padded[offset : offset + length]
    return summed


def split_dot(spec, table, values):
    high = lax.reduce_precision(table, exponent_bits=8, mantissa_bits=7)
    low = (table - high).astype(jnp.bfloat16)
    lhs = jnp.einsum(spec, high.astype(jnp.bfloat16), values, preferred_element_type=jnp.float32)
    return lhs + jnp.einsum(spec, low, values, preferred_element_type=jnp.float32)


def cube_coefficients(size, index):
    terms = []
    shift = 1
    while shift < size:
        offset = (index % shift).astype(jnp.float32)
        terms += [jnp.float32(shift), offset, shift - 1 - offset]
        shift *= 2
    return terms


def cube_weights(factors, size, index):
    rounds = []
    shift = 1
    step = 0
    while shift < size:
        upper = (index & shift) != 0
        span, lead, trail = factors[step], factors[step + 1], factors[step + 2]
        one = jnp.ones_like(span)
        zero = jnp.zeros_like(span)
        keep = jnp.stack([jnp.where(upper, one, span), jnp.where(upper, span, one)])
        take = jnp.stack([jnp.where(upper, span, one), jnp.where(upper, one, span)])
        add = jnp.stack([jnp.where(upper, lead, zero), jnp.where(upper, zero, trail)])
        rounds.append((keep, take, add))
        shift *= 2
        step += 3
    return rounds


def cube_scan(window, rounds, axis, size, held, hold_at=1):
    entering = jnp.zeros_like(window)
    shift = 1
    for keep, take, add in rounds:
        arrived = lax.ppermute(window, axis, [(source, source ^ shift) for source in range(size)])
        if shift == hold_at:
            held, arrived = lax.optimization_barrier((held, arrived))
        entering = entering + add * arrived
        window = keep * window + take * arrived
        shift *= 2
    return entering, window, held


def shards(inner, u_query, u_key, u_value, short_filter, decay_rate, residue, grad_out):
    block_len, channels = u_query.shape
    group_count = channels // GROUP
    rim_rows = jnp.stack(
        [
            u_query[block_len - SHORT + 1 :],
            u_key[block_len - SHORT + 1 :],
            u_value[block_len - SHORT + 1 :],
        ]
    )
    before = from_behind(rim_rows, ("zl", "xc"), 1)
    q_short = rounded(short_causal(before[0], u_query, short_filter[0]))
    k_short = rounded(short_causal(before[1], u_key, short_filter[1]))
    v_short = rounded(short_causal(before[2], u_value, short_filter[2]))
    product = rounded(k_short.astype(jnp.float32) * v_short.astype(jnp.float32))
    grad_conv = rounded(grad_out.astype(jnp.float32) * q_short.astype(jnp.float32))

    rates = decay_rate
    weights = residue * jnp.sqrt(-jnp.expm1(-2.0 * rates))
    lags = jnp.arange(block_len + 1).astype(jnp.float32)
    powers = jnp.exp(-rates[:, :, None] * lags)

    signal = product.reshape(block_len, group_count, GROUP)
    cotangent = grad_conv.reshape(block_len, group_count, GROUP)
    order = rates.shape[1]
    owner = (jnp.arange(channels) // GROUP)[None, :] == jnp.arange(group_count)[:, None]
    owner = owner.astype(jnp.float32)

    def own_block(full):
        return (full.reshape(group_count, order, channels) * owner[:, None, :]).sum(0)

    def spread(state):
        return (state[None] * owner[:, None, :]).reshape(group_count * order, channels)

    end_rows = powers[:, :, block_len - 1 :: -1].reshape(group_count * order, block_len)
    start_rows = powers[:, :, :block_len].reshape(group_count * order, block_len)
    end_state = own_block(split_dot("ks,sc->kc", end_rows, product))
    start_state = own_block(split_dot("ks,sc->kc", start_rows, grad_conv))
    decay_step = jnp.repeat(rates.T, GROUP, axis=1) * block_len
    member = lax.axis_index("xc")
    outer = lax.axis_size("zl")
    band = lax.axis_index("zl")
    place = member.astype(jnp.float32)
    inner_terms = cube_coefficients(inner, member)
    outer_terms = [inner * term for term in cube_coefficients(outer, band)]
    unit_terms = [place, inner - 1 - place, jnp.float32(1), jnp.float32(-1)]
    terms = jnp.stack(inner_terms + outer_terms + unit_terms)
    factors = jnp.exp(-decay_step[None] * terms[:, None, None])
    inner_rounds = cube_weights(factors, inner, member)
    outer_rounds = cube_weights(factors[len(inner_terms) :], outer, band)
    near, group, (rates, weights) = cube_scan(
        jnp.stack([end_state, start_state]), inner_rounds, "xc", inner, (rates, weights), 2
    )
    far, _, _ = cube_scan(group, outer_rounds, "zl", outer, ())
    entering = near[0] + factors[-4] * far[0]
    leaving = near[1] + factors[-3] * far[1]

    centred = jnp.arange(block_len).astype(jnp.float32) - block_len // 2
    falling = weights[:, None, :] * jnp.exp(-centred[None, :, None] * rates[:, None, :])
    rising = jnp.exp(centred[None, None, :] * rates[:, :, None])
    toeplitz = jnp.einsum("gtm,gms->gts", falling, rising, precision=precise)
    lower = jnp.arange(block_len)[:, None] >= jnp.arange(block_len)[None, :]
    toeplitz = jnp.where(lower[None], toeplitz, 0.0)
    local_conv = split_dot("gts,sgc->tgc", toeplitz, signal).reshape(block_len, channels)
    local_grad = split_dot("gts,tgc->sgc", toeplitz, cotangent).reshape(block_len, channels)
    lead_fwd = (weights[:, :, None] * powers[:, :, 1:]).reshape(group_count * order, block_len)
    lead_bwd = (weights[:, :, None] * powers[:, :, block_len:0:-1]).reshape(
        group_count * order, block_len
    )
    carried_conv = jnp.einsum("kt,kc->tc", lead_fwd, spread(entering), precision=precise)
    carried_grad = jnp.einsum("ks,kc->sc", lead_bwd, spread(leaving), precision=precise)
    conv_out = rounded(local_conv + carried_conv)
    grad_prod = rounded(local_grad + carried_grad)

    edge = SHORT - 1
    ahead = jnp.concatenate(
        [
            local_conv[:edge],
            local_grad[:edge],
            grad_out[:edge].astype(jnp.float32),
            k_short[:edge].astype(jnp.float32),
            v_short[:edge].astype(jnp.float32),
            start_state,
        ]
    )
    ahead = from_behind(ahead, ("zl", "xc"), -1)
    through = factors[-2] * entering + end_state
    beyond = (leaving - ahead[5 * edge :]) * factors[-1]
    next_conv = rounded(
        ahead[:edge]
        + jnp.einsum("kt,kc->tc", lead_fwd[:, :edge], spread(through), precision=precise)
    )
    next_grad = rounded(
        ahead[edge : 2 * edge]
        + jnp.einsum("ks,kc->sc", lead_bwd[:, :edge], spread(beyond), precision=precise)
    )
    next_rows = (
        rounded(ahead[2 * edge : 3 * edge] * next_conv.astype(jnp.float32)),
        rounded(next_grad.astype(jnp.float32) * ahead[4 * edge : 5 * edge]),
        rounded(next_grad.astype(jnp.float32) * ahead[3 * edge : 4 * edge]),
    )

    mixer_out = (q_short.astype(jnp.float32) * conv_out.astype(jnp.float32)).astype(jnp.bfloat16)
    grad_qshort = rounded(grad_out.astype(jnp.float32) * conv_out.astype(jnp.float32))
    grad_kshort = rounded(grad_prod.astype(jnp.float32) * v_short.astype(jnp.float32))
    grad_vshort = rounded(grad_prod.astype(jnp.float32) * k_short.astype(jnp.float32))
    grad_query = short_reverse(grad_qshort, next_rows[0], short_filter[0]).astype(jnp.bfloat16)
    grad_key = short_reverse(grad_kshort, next_rows[1], short_filter[1]).astype(jnp.bfloat16)
    grad_value = short_reverse(grad_vshort, next_rows[2], short_filter[2]).astype(jnp.bfloat16)
    return (mixer_out, grad_query, grad_key, grad_value)


def solution(mesh):
    ctx_count = mesh.shape["ctx"]
    inner = math.gcd(INNER, ctx_count)
    grid = Mesh(
        mesh.devices.reshape(ctx_count // inner, inner, mesh.shape["tp"]), ("zl", "xc", "tp")
    )
    rows = P(("zl", "xc"), "tp")
    return jax.shard_map(
        lambda *arrays: shards(inner, *arrays),
        mesh=grid,
        in_specs=(rows, rows, rows, P(None, None, "tp"), P("tp", None), P("tp", None), rows),
        out_specs=(rows, rows, rows, rows),
        check_vma=False,
    )
```

```python
import math

import jax
import jax.numpy as jnp
from jax import lax
from jax.sharding import Mesh, PartitionSpec as P

GROUP = 16
SHORT = 7
INNER = 8


precise = lax.Precision.HIGHEST


def from_behind(value, axis, steps):
    count = lax.axis_size(axis)
    leading, last = (max(0, -steps), min(count, count - steps))
    return lax.ppermute(value, axis, [(source, source + steps) for source in range(leading, last)])


def rounded(values):
    return lax.optimization_barrier(values.astype(jnp.bfloat16))


def short_causal(prior_rows, inputs, filter_taps):
    length = inputs.shape[0]
    padded = jnp.concatenate([prior_rows.astype(jnp.float32), inputs.astype(jnp.float32)], axis=0)
    summed = jnp.zeros(inputs.shape, jnp.float32)
    for offset in range(SHORT):
        summed = (
            summed + filter_taps[offset] * padded[SHORT - 1 - offset : SHORT - 1 - offset + length]
        )
    return summed


def short_reverse(grad_rows, next_rows, filter_taps):
    length = grad_rows.shape[0]
    padded = jnp.concatenate([grad_rows.astype(jnp.float32), next_rows.astype(jnp.float32)], axis=0)
    summed = jnp.zeros(grad_rows.shape, jnp.float32)
    for offset in range(SHORT):
        summed = summed + filter_taps[offset] * padded[offset : offset + length]
    return summed


def split_dot(spec, table, values):
    high = lax.reduce_precision(table, exponent_bits=8, mantissa_bits=7)
    low = (table - high).astype(jnp.bfloat16)
    lhs = jnp.einsum(spec, high.astype(jnp.bfloat16), values, preferred_element_type=jnp.float32)
    return lhs + jnp.einsum(spec, low, values, preferred_element_type=jnp.float32)


def cube_coefficients(size, index):
    terms = []
    shift = 1
    while shift < size:
        offset = (index % shift).astype(jnp.float32)
        terms += [jnp.float32(shift), offset, shift - 1 - offset]
        shift *= 2
    return terms


def cube_weights(factors, size, index):
    rounds = []
    shift = 1
    step = 0
    while shift < size:
        upper = (index & shift) != 0
        span, lead, trail = factors[step], factors[step + 1], factors[step + 2]
        one = jnp.ones_like(span)
        zero = jnp.zeros_like(span)
        keep = jnp.stack([jnp.where(upper, one, span), jnp.where(upper, span, one)])
        take = jnp.stack([jnp.where(upper, span, one), jnp.where(upper, one, span)])
        add = jnp.stack([jnp.where(upper, lead, zero), jnp.where(upper, zero, trail)])
        rounds.append((keep, take, add))
        shift *= 2
        step += 3
    return rounds


def cube_scan(window, rounds, axis, size, held):
    entering = jnp.zeros_like(window)
    shift = 1
    for keep, take, add in rounds:
        arrived = lax.ppermute(window, axis, [(source, source ^ shift) for source in range(size)])
        if shift == 1:
            held, arrived = lax.optimization_barrier((held, arrived))
        entering = entering + add * arrived
        window = keep * window + take * arrived
        shift *= 2
    return entering, window, held


def shards(inner, u_query, u_key, u_value, short_filter, decay_rate, residue, grad_out):
    block_len, channels = u_query.shape
    group_count = channels // GROUP
    rim_rows = jnp.stack(
        [
            u_query[block_len - SHORT + 1 :],
            u_key[block_len - SHORT + 1 :],
            u_value[block_len - SHORT + 1 :],
        ]
    )
    before = from_behind(rim_rows, ("zl", "xc"), 1)
    q_short = short_causal(before[0], u_query, short_filter[0]).astype(jnp.bfloat16)
    k_short = short_causal(before[1], u_key, short_filter[1]).astype(jnp.bfloat16)
    v_short = short_causal(before[2], u_value, short_filter[2]).astype(jnp.bfloat16)
    product = rounded(k_short.astype(jnp.float32) * v_short.astype(jnp.float32))
    grad_conv = rounded(grad_out.astype(jnp.float32) * q_short.astype(jnp.float32))

    rates = decay_rate
    weights = residue * jnp.sqrt(-jnp.expm1(-2.0 * rates))
    lags = jnp.arange(block_len + 1).astype(jnp.float32)
    powers = jnp.exp(-rates[:, :, None] * lags)

    signal = product.reshape(block_len, group_count, GROUP)
    cotangent = grad_conv.reshape(block_len, group_count, GROUP)
    order = rates.shape[1]
    owner = (jnp.arange(channels) // GROUP)[None, :] == jnp.arange(group_count)[:, None]
    owner = owner.astype(jnp.float32)

    def own_block(full):
        return (full.reshape(group_count, order, channels) * owner[:, None, :]).sum(0)

    def spread(state):
        return (state[None] * owner[:, None, :]).reshape(group_count * order, channels)

    end_rows = powers[:, :, block_len - 1 :: -1].reshape(group_count * order, block_len)
    start_rows = powers[:, :, :block_len].reshape(group_count * order, block_len)
    end_state = own_block(split_dot("ks,sc->kc", end_rows, product))
    start_state = own_block(split_dot("ks,sc->kc", start_rows, grad_conv))
    decay_step = jnp.repeat(rates.T, GROUP, axis=1) * block_len
    member = lax.axis_index("xc")
    outer = lax.axis_size("zl")
    band = lax.axis_index("zl")
    place = member.astype(jnp.float32)
    inner_terms = cube_coefficients(inner, member)
    outer_terms = [inner * term for term in cube_coefficients(outer, band)]
    unit_terms = [place, inner - 1 - place, jnp.float32(1), jnp.float32(-1)]
    terms = jnp.stack(inner_terms + outer_terms + unit_terms)
    factors = jnp.exp(-decay_step[None] * terms[:, None, None])
    inner_rounds = cube_weights(factors, inner, member)
    outer_rounds = cube_weights(factors[len(inner_terms) :], outer, band)
    near, group, (rates, weights) = cube_scan(
        jnp.stack([end_state, start_state]), inner_rounds, "xc", inner, (rates, weights)
    )
    far, _, _ = cube_scan(group, outer_rounds, "zl", outer, ())
    entering = near[0] + factors[-4] * far[0]
    leaving = near[1] + factors[-3] * far[1]

    centred = jnp.arange(block_len).astype(jnp.float32) - block_len // 2
    falling = weights[:, None, :] * jnp.exp(-centred[None, :, None] * rates[:, None, :])
    rising = jnp.exp(centred[None, None, :] * rates[:, :, None])
    toeplitz = jnp.einsum("gtm,gms->gts", falling, rising, precision=precise)
    lower = jnp.arange(block_len)[:, None] >= jnp.arange(block_len)[None, :]
    toeplitz = jnp.where(lower[None], toeplitz, 0.0)
    local_conv = split_dot("gts,sgc->tgc", toeplitz, signal).reshape(block_len, channels)
    local_grad = split_dot("gts,tgc->sgc", toeplitz, cotangent).reshape(block_len, channels)
    lead_fwd = (weights[:, :, None] * powers[:, :, 1:]).reshape(group_count * order, block_len)
    lead_bwd = (weights[:, :, None] * powers[:, :, block_len:0:-1]).reshape(
        group_count * order, block_len
    )
    carried_conv = jnp.einsum("kt,kc->tc", lead_fwd, spread(entering), precision=precise)
    carried_grad = jnp.einsum("ks,kc->sc", lead_bwd, spread(leaving), precision=precise)
    conv_out = rounded(local_conv + carried_conv)
    grad_prod = rounded(local_grad + carried_grad)

    edge = SHORT - 1
    ahead = jnp.concatenate(
        [
            local_conv[:edge],
            local_grad[:edge],
            grad_out[:edge].astype(jnp.float32),
            k_short[:edge].astype(jnp.float32),
            v_short[:edge].astype(jnp.float32),
            start_state,
        ]
    )
    ahead = from_behind(ahead, ("zl", "xc"), -1)
    through = factors[-2] * entering + end_state
    beyond = (leaving - ahead[5 * edge :]) * factors[-1]
    next_conv = rounded(
        ahead[:edge]
        + jnp.einsum("kt,kc->tc", lead_fwd[:, :edge], spread(through), precision=precise)
    )
    next_grad = rounded(
        ahead[edge : 2 * edge]
        + jnp.einsum("ks,kc->sc", lead_bwd[:, :edge], spread(beyond), precision=precise)
    )
    next_rows = (
        rounded(ahead[2 * edge : 3 * edge] * next_conv.astype(jnp.float32)),
        rounded(next_grad.astype(jnp.float32) * ahead[4 * edge : 5 * edge]),
        rounded(next_grad.astype(jnp.float32) * ahead[3 * edge : 4 * edge]),
    )

    mixer_out = (q_short.astype(jnp.float32) * conv_out.astype(jnp.float32)).astype(jnp.bfloat16)
    grad_qshort = rounded(grad_out.astype(jnp.float32) * conv_out.astype(jnp.float32))
    grad_kshort = rounded(grad_prod.astype(jnp.float32) * v_short.astype(jnp.float32))
    grad_vshort = rounded(grad_prod.astype(jnp.float32) * k_short.astype(jnp.float32))
    grad_query = short_reverse(grad_qshort, next_rows[0], short_filter[0]).astype(jnp.bfloat16)
    grad_key = short_reverse(grad_kshort, next_rows[1], short_filter[1]).astype(jnp.bfloat16)
    grad_value = short_reverse(grad_vshort, next_rows[2], short_filter[2]).astype(jnp.bfloat16)
    return (mixer_out, grad_query, grad_key, grad_value)


def solution(mesh):
    ctx_count = mesh.shape["ctx"]
    inner = math.gcd(INNER, ctx_count)
    grid = Mesh(
        mesh.devices.reshape(ctx_count // inner, inner, mesh.shape["tp"]), ("zl", "xc", "tp")
    )
    rows = P(("zl", "xc"), "tp")
    return jax.shard_map(
        lambda *arrays: shards(inner, *arrays),
        mesh=grid,
        in_specs=(rows, rows, rows, P(None, None, "tp"), P("tp", None), P("tp", None), rows),
        out_specs=(rows, rows, rows, rows),
        check_vma=False,
    )
```

```python
import math

import jax
import jax.numpy as jnp
from jax import lax
from jax.sharding import Mesh, PartitionSpec as P

GROUP = 16
SHORT = 7
INNER = 8


precise = lax.Precision.HIGHEST


def from_behind(value, axis, steps):
    count = lax.axis_size(axis)
    leading, last = (max(0, -steps), min(count, count - steps))
    return lax.ppermute(value, axis, [(source, source + steps) for source in range(leading, last)])


def rounded(values):
    return lax.optimization_barrier(values.astype(jnp.bfloat16))


def to_bf16(values):
    return lax.reduce_precision(values, exponent_bits=8, mantissa_bits=7).astype(jnp.bfloat16)


def short_causal(prior_rows, inputs, filter_taps):
    length = inputs.shape[0]
    padded = jnp.concatenate([prior_rows.astype(jnp.float32), inputs.astype(jnp.float32)], axis=0)
    summed = jnp.zeros(inputs.shape, jnp.float32)
    for offset in range(SHORT):
        summed = (
            summed + filter_taps[offset] * padded[SHORT - 1 - offset : SHORT - 1 - offset + length]
        )
    return summed


def short_reverse(grad_rows, next_rows, filter_taps):
    length = grad_rows.shape[0]
    padded = jnp.concatenate([grad_rows.astype(jnp.float32), next_rows.astype(jnp.float32)], axis=0)
    summed = jnp.zeros(grad_rows.shape, jnp.float32)
    for offset in range(SHORT):
        summed = summed + filter_taps[offset] * padded[offset : offset + length]
    return summed


def split_dot(spec, table, values):
    high = lax.reduce_precision(table, exponent_bits=8, mantissa_bits=7)
    low = (table - high).astype(jnp.bfloat16)
    lhs = jnp.einsum(spec, high.astype(jnp.bfloat16), values, preferred_element_type=jnp.float32)
    return lhs + jnp.einsum(spec, low, values, preferred_element_type=jnp.float32)


def cube_coefficients(size, index):
    terms = []
    shift = 1
    while shift < size:
        offset = (index % shift).astype(jnp.float32)
        terms += [jnp.float32(shift), offset, shift - 1 - offset]
        shift *= 2
    return terms


def cube_weights(factors, size, index):
    rounds = []
    shift = 1
    step = 0
    while shift < size:
        upper = (index & shift) != 0
        span, lead, trail = factors[step], factors[step + 1], factors[step + 2]
        one = jnp.ones_like(span)
        zero = jnp.zeros_like(span)
        keep = jnp.stack([jnp.where(upper, one, span), jnp.where(upper, span, one)])
        take = jnp.stack([jnp.where(upper, span, one), jnp.where(upper, one, span)])
        add = jnp.stack([jnp.where(upper, lead, zero), jnp.where(upper, zero, trail)])
        rounds.append((keep, take, add))
        shift *= 2
        step += 3
    return rounds


def cube_scan(window, rounds, axis, size, held):
    entering = jnp.zeros_like(window)
    shift = 1
    for keep, take, add in rounds:
        arrived = lax.ppermute(window, axis, [(source, source ^ shift) for source in range(size)])
        if shift == 1:
            held, arrived = lax.optimization_barrier((held, arrived))
        entering = entering + add * arrived
        window = keep * window + take * arrived
        shift *= 2
    return entering, window, held


def shards(inner, u_query, u_key, u_value, short_filter, decay_rate, residue, grad_out):
    block_len, channels = u_query.shape
    group_count = channels // GROUP
    rim_rows = jnp.stack(
        [
            u_query[block_len - SHORT + 1 :],
            u_key[block_len - SHORT + 1 :],
            u_value[block_len - SHORT + 1 :],
        ]
    )
    before = from_behind(rim_rows, ("zl", "xc"), 1)
    q_short = to_bf16(short_causal(before[0], u_query, short_filter[0]))
    k_short = to_bf16(short_causal(before[1], u_key, short_filter[1]))
    v_short = to_bf16(short_causal(before[2], u_value, short_filter[2]))
    product = rounded(k_short.astype(jnp.float32) * v_short.astype(jnp.float32))
    grad_conv = rounded(grad_out.astype(jnp.float32) * q_short.astype(jnp.float32))

    rates = decay_rate
    weights = residue * jnp.sqrt(-jnp.expm1(-2.0 * rates))
    lags = jnp.arange(block_len + 1).astype(jnp.float32)
    powers = jnp.exp(-rates[:, :, None] * lags)

    signal = product.reshape(block_len, group_count, GROUP)
    cotangent = grad_conv.reshape(block_len, group_count, GROUP)
    order = rates.shape[1]
    owner = (jnp.arange(channels) // GROUP)[None, :] == jnp.arange(group_count)[:, None]
    owner = owner.astype(jnp.float32)

    def own_block(full):
        return (full.reshape(group_count, order, channels) * owner[:, None, :]).sum(0)

    def spread(state):
        return (state[None] * owner[:, None, :]).reshape(group_count * order, channels)

    end_rows = powers[:, :, block_len - 1 :: -1].reshape(group_count * order, block_len)
    start_rows = powers[:, :, :block_len].reshape(group_count * order, block_len)
    end_state = own_block(split_dot("ks,sc->kc", end_rows, product))
    start_state = own_block(split_dot("ks,sc->kc", start_rows, grad_conv))
    decay_step = jnp.repeat(rates.T, GROUP, axis=1) * block_len
    member = lax.axis_index("xc")
    outer = lax.axis_size("zl")
    band = lax.axis_index("zl")
    place = member.astype(jnp.float32)
    inner_terms = cube_coefficients(inner, member)
    outer_terms = [inner * term for term in cube_coefficients(outer, band)]
    unit_terms = [place, inner - 1 - place, jnp.float32(1), jnp.float32(-1)]
    terms = jnp.stack(inner_terms + outer_terms + unit_terms)
    factors = jnp.exp(-decay_step[None] * terms[:, None, None])
    inner_rounds = cube_weights(factors, inner, member)
    outer_rounds = cube_weights(factors[len(inner_terms) :], outer, band)
    near, group, (rates, weights) = cube_scan(
        jnp.stack([end_state, start_state]), inner_rounds, "xc", inner, (rates, weights)
    )
    far, _, _ = cube_scan(group, outer_rounds, "zl", outer, ())
    entering = near[0] + factors[-4] * far[0]
    leaving = near[1] + factors[-3] * far[1]

    centred = jnp.arange(block_len).astype(jnp.float32) - block_len // 2
    falling = weights[:, None, :] * jnp.exp(-centred[None, :, None] * rates[:, None, :])
    rising = jnp.exp(centred[None, None, :] * rates[:, :, None])
    toeplitz = jnp.einsum("gtm,gms->gts", falling, rising, precision=precise)
    lower = jnp.arange(block_len)[:, None] >= jnp.arange(block_len)[None, :]
    toeplitz = jnp.where(lower[None], toeplitz, 0.0)
    local_conv = split_dot("gts,sgc->tgc", toeplitz, signal).reshape(block_len, channels)
    local_grad = split_dot("gts,tgc->sgc", toeplitz, cotangent).reshape(block_len, channels)
    lead_fwd = (weights[:, :, None] * powers[:, :, 1:]).reshape(group_count * order, block_len)
    lead_bwd = (weights[:, :, None] * powers[:, :, block_len:0:-1]).reshape(
        group_count * order, block_len
    )
    carried_conv = jnp.einsum("kt,kc->tc", lead_fwd, spread(entering), precision=precise)
    carried_grad = jnp.einsum("ks,kc->sc", lead_bwd, spread(leaving), precision=precise)
    conv_out = rounded(local_conv + carried_conv)
    grad_prod = rounded(local_grad + carried_grad)

    edge = SHORT - 1
    ahead = jnp.concatenate(
        [
            local_conv[:edge],
            local_grad[:edge],
            grad_out[:edge].astype(jnp.float32),
            k_short[:edge].astype(jnp.float32),
            v_short[:edge].astype(jnp.float32),
            start_state,
        ]
    )
    ahead = from_behind(ahead, ("zl", "xc"), -1)
    through = factors[-2] * entering + end_state
    beyond = (leaving - ahead[5 * edge :]) * factors[-1]
    next_conv = rounded(
        ahead[:edge]
        + jnp.einsum("kt,kc->tc", lead_fwd[:, :edge], spread(through), precision=precise)
    )
    next_grad = rounded(
        ahead[edge : 2 * edge]
        + jnp.einsum("ks,kc->sc", lead_bwd[:, :edge], spread(beyond), precision=precise)
    )
    next_rows = (
        rounded(ahead[2 * edge : 3 * edge] * next_conv.astype(jnp.float32)),
        rounded(next_grad.astype(jnp.float32) * ahead[4 * edge : 5 * edge]),
        rounded(next_grad.astype(jnp.float32) * ahead[3 * edge : 4 * edge]),
    )

    mixer_out = (q_short.astype(jnp.float32) * conv_out.astype(jnp.float32)).astype(jnp.bfloat16)
    grad_qshort = rounded(grad_out.astype(jnp.float32) * conv_out.astype(jnp.float32))
    grad_kshort = rounded(grad_prod.astype(jnp.float32) * v_short.astype(jnp.float32))
    grad_vshort = rounded(grad_prod.astype(jnp.float32) * k_short.astype(jnp.float32))
    grad_query = short_reverse(grad_qshort, next_rows[0], short_filter[0]).astype(jnp.bfloat16)
    grad_key = short_reverse(grad_kshort, next_rows[1], short_filter[1]).astype(jnp.bfloat16)
    grad_value = short_reverse(grad_vshort, next_rows[2], short_filter[2]).astype(jnp.bfloat16)
    return (mixer_out, grad_query, grad_key, grad_value)


def solution(mesh):
    ctx_count = mesh.shape["ctx"]
    inner = math.gcd(INNER, ctx_count)
    grid = Mesh(
        mesh.devices.reshape(ctx_count // inner, inner, mesh.shape["tp"]), ("zl", "xc", "tp")
    )
    rows = P(("zl", "xc"), "tp")
    return jax.shard_map(
        lambda *arrays: shards(inner, *arrays),
        mesh=grid,
        in_specs=(rows, rows, rows, P(None, None, "tp"), P("tp", None), P("tp", None), rows),
        out_specs=(rows, rows, rows, rows),
        check_vma=False,
    )
```

```python
import math

import jax
import jax.numpy as jnp
from jax import lax
from jax.sharding import Mesh, PartitionSpec as P

GROUP = 16
SHORT = 7
INNER = 8


precise = lax.Precision.HIGHEST


def from_behind(value, axis, steps):
    count = lax.axis_size(axis)
    leading, last = (max(0, -steps), min(count, count - steps))
    return lax.ppermute(value, axis, [(source, source + steps) for source in range(leading, last)])


def rounded(values):
    return lax.optimization_barrier(values.astype(jnp.bfloat16))


def to_bf16(values):
    return lax.reduce_precision(values, exponent_bits=8, mantissa_bits=7).astype(jnp.bfloat16)


def short_causal(prior_rows, inputs, filter_taps):
    length = inputs.shape[0]
    padded = jnp.concatenate([prior_rows.astype(jnp.float32), inputs.astype(jnp.float32)], axis=0)
    summed = jnp.zeros(inputs.shape, jnp.float32)
    for offset in range(SHORT):
        summed = (
            summed + filter_taps[offset] * padded[SHORT - 1 - offset : SHORT - 1 - offset + length]
        )
    return summed


def short_reverse(grad_rows, next_rows, filter_taps):
    length = grad_rows.shape[0]
    padded = jnp.concatenate([grad_rows.astype(jnp.float32), next_rows.astype(jnp.float32)], axis=0)
    summed = jnp.zeros(grad_rows.shape, jnp.float32)
    for offset in range(SHORT):
        summed = summed + filter_taps[offset] * padded[offset : offset + length]
    return summed


def split_dot(spec, table, values):
    high = lax.reduce_precision(table, exponent_bits=8, mantissa_bits=7)
    low = (table - high).astype(jnp.bfloat16)
    lhs = jnp.einsum(spec, high.astype(jnp.bfloat16), values, preferred_element_type=jnp.float32)
    return lhs + jnp.einsum(spec, low, values, preferred_element_type=jnp.float32)


def cube_coefficients(size, index):
    terms = []
    shift = 1
    while shift < size:
        offset = (index % shift).astype(jnp.float32)
        terms += [jnp.float32(shift), offset, shift - 1 - offset]
        shift *= 2
    return terms


def cube_weights(factors, size, index):
    rounds = []
    shift = 1
    step = 0
    while shift < size:
        upper = (index & shift) != 0
        span, lead, trail = factors[step], factors[step + 1], factors[step + 2]
        one = jnp.ones_like(span)
        zero = jnp.zeros_like(span)
        keep = jnp.stack([jnp.where(upper, one, span), jnp.where(upper, span, one)])
        take = jnp.stack([jnp.where(upper, span, one), jnp.where(upper, one, span)])
        add = jnp.stack([jnp.where(upper, lead, zero), jnp.where(upper, zero, trail)])
        rounds.append((keep, take, add))
        shift *= 2
        step += 3
    return rounds


def cube_scan(window, rounds, axis, size, held):
    entering = jnp.zeros_like(window)
    shift = 1
    for keep, take, add in rounds:
        arrived = lax.ppermute(window, axis, [(source, source ^ shift) for source in range(size)])
        if shift == 1:
            held, arrived = lax.optimization_barrier((held, arrived))
        entering = entering + add * arrived
        window = keep * window + take * arrived
        shift *= 2
    return entering, window, held


def shards(inner, u_query, u_key, u_value, short_filter, decay_rate, residue, grad_out):
    block_len, channels = u_query.shape
    group_count = channels // GROUP
    rim_rows = jnp.stack(
        [
            u_query[block_len - SHORT + 1 :],
            u_key[block_len - SHORT + 1 :],
            u_value[block_len - SHORT + 1 :],
        ]
    )
    before = from_behind(rim_rows, ("zl", "xc"), 1)
    q_short = to_bf16(short_causal(before[0], u_query, short_filter[0]))
    k_short = to_bf16(short_causal(before[1], u_key, short_filter[1]))
    v_short = to_bf16(short_causal(before[2], u_value, short_filter[2]))
    product = rounded(k_short.astype(jnp.float32) * v_short.astype(jnp.float32))
    grad_conv = rounded(grad_out.astype(jnp.float32) * q_short.astype(jnp.float32))

    rates = decay_rate
    weights = residue * jnp.sqrt(-jnp.expm1(-2.0 * rates))
    lags = jnp.arange(block_len + 1).astype(jnp.float32)
    powers = jnp.exp(-rates[:, :, None] * lags)

    signal = product.reshape(block_len, group_count, GROUP)
    cotangent = grad_conv.reshape(block_len, group_count, GROUP)
    order = rates.shape[1]
    owner = (jnp.arange(channels) // GROUP)[None, :] == jnp.arange(group_count)[:, None]
    owner = owner.astype(jnp.float32)

    def own_block(full):
        return (full.reshape(group_count, order, channels) * owner[:, None, :]).sum(0)

    def spread(state):
        return (state[None] * owner[:, None, :]).reshape(group_count * order, channels)

    end_rows = powers[:, :, block_len - 1 :: -1].reshape(group_count * order, block_len)
    start_rows = powers[:, :, :block_len].reshape(group_count * order, block_len)
    end_state = own_block(split_dot("ks,sc->kc", end_rows, product))
    start_state = own_block(split_dot("ks,sc->kc", start_rows, grad_conv))
    decay_step = jnp.repeat(rates.T, GROUP, axis=1) * block_len
    member = lax.axis_index("xc")
    outer = lax.axis_size("zl")
    band = lax.axis_index("zl")
    place = member.astype(jnp.float32)
    inner_terms = cube_coefficients(inner, member)
    outer_terms = [inner * term for term in cube_coefficients(outer, band)]
    unit_terms = [place, inner - 1 - place, jnp.float32(1), jnp.float32(-1)]
    terms = jnp.stack(inner_terms + outer_terms + unit_terms)
    factors = jnp.exp(-decay_step[None] * terms[:, None, None])
    inner_rounds = cube_weights(factors, inner, member)
    outer_rounds = cube_weights(factors[len(inner_terms) :], outer, band)
    near, group, (rates, weights) = cube_scan(
        jnp.stack([end_state, start_state]), inner_rounds, "xc", inner, (rates, weights)
    )
    far, _, _ = cube_scan(group, outer_rounds, "zl", outer, ())
    entering = near[0] + factors[-4] * far[0]
    leaving = near[1] + factors[-3] * far[1]

    centred = jnp.arange(block_len).astype(jnp.float32) - block_len // 2
    falling = weights[:, None, :] * jnp.exp(-centred[None, :, None] * rates[:, None, :])
    rising = jnp.exp(centred[None, None, :] * rates[:, :, None])
    toeplitz = jnp.einsum("gtm,gms->gts", falling, rising, precision=precise)
    lower = jnp.arange(block_len)[:, None] >= jnp.arange(block_len)[None, :]
    toeplitz = jnp.where(lower[None], toeplitz, 0.0)
    local_conv = split_dot("gts,sgc->tgc", toeplitz, signal).reshape(block_len, channels)
    local_grad = split_dot("gts,tgc->sgc", toeplitz, cotangent).reshape(block_len, channels)
    lead_fwd = (weights[:, :, None] * powers[:, :, 1:]).reshape(group_count * order, block_len)
    lead_bwd = (weights[:, :, None] * powers[:, :, block_len:0:-1]).reshape(
        group_count * order, block_len
    )
    carried_conv = jnp.einsum("kt,kc->tc", lead_fwd, spread(entering), precision=precise)
    carried_grad = jnp.einsum("ks,kc->sc", lead_bwd, spread(leaving), precision=precise)
    conv_out = rounded(local_conv + carried_conv)
    grad_prod = rounded(local_grad + carried_grad)

    edge = SHORT - 1
    ahead = jnp.concatenate(
        [
            local_conv[:edge],
            local_grad[:edge],
            grad_out[:edge].astype(jnp.float32),
            k_short[:edge].astype(jnp.float32),
            v_short[:edge].astype(jnp.float32),
            start_state,
        ]
    )
    ahead = from_behind(ahead, ("zl", "xc"), -1)
    through = factors[-2] * entering + end_state
    beyond = (leaving - ahead[5 * edge :]) * factors[-1]
    next_conv = rounded(
        ahead[:edge]
        + jnp.einsum("kt,kc->tc", lead_fwd[:, :edge], spread(through), precision=precise)
    )
    next_grad = rounded(
        ahead[edge : 2 * edge]
        + jnp.einsum("ks,kc->sc", lead_bwd[:, :edge], spread(beyond), precision=precise)
    )
    next_rows = (
        rounded(ahead[2 * edge : 3 * edge] * next_conv.astype(jnp.float32)),
        rounded(next_grad.astype(jnp.float32) * ahead[4 * edge : 5 * edge]),
        rounded(next_grad.astype(jnp.float32) * ahead[3 * edge : 4 * edge]),
    )

    mixer_out = (q_short.astype(jnp.float32) * conv_out.astype(jnp.float32)).astype(jnp.bfloat16)
    grad_qshort = to_bf16(grad_out.astype(jnp.float32) * conv_out.astype(jnp.float32))
    grad_kshort = to_bf16(grad_prod.astype(jnp.float32) * v_short.astype(jnp.float32))
    grad_vshort = to_bf16(grad_prod.astype(jnp.float32) * k_short.astype(jnp.float32))
    grad_query = short_reverse(grad_qshort, next_rows[0], short_filter[0]).astype(jnp.bfloat16)
    grad_key = short_reverse(grad_kshort, next_rows[1], short_filter[1]).astype(jnp.bfloat16)
    grad_value = short_reverse(grad_vshort, next_rows[2], short_filter[2]).astype(jnp.bfloat16)
    return (mixer_out, grad_query, grad_key, grad_value)


def solution(mesh):
    ctx_count = mesh.shape["ctx"]
    inner = math.gcd(INNER, ctx_count)
    grid = Mesh(
        mesh.devices.reshape(ctx_count // inner, inner, mesh.shape["tp"]), ("zl", "xc", "tp")
    )
    rows = P(("zl", "xc"), "tp")
    return jax.shard_map(
        lambda *arrays: shards(inner, *arrays),
        mesh=grid,
        in_specs=(rows, rows, rows, P(None, None, "tp"), P("tp", None), P("tp", None), rows),
        out_specs=(rows, rows, rows, rows),
        check_vma=False,
    )
```

```python
import math

import jax
import jax.numpy as jnp
from jax import lax
from jax.sharding import Mesh, PartitionSpec as P

GROUP = 16
SHORT = 7
INNER = 8


precise = lax.Precision.HIGHEST


def from_behind(value, axis, steps):
    count = lax.axis_size(axis)
    leading, last = (max(0, -steps), min(count, count - steps))
    return lax.ppermute(value, axis, [(source, source + steps) for source in range(leading, last)])


def rounded(values):
    return lax.optimization_barrier(values.astype(jnp.bfloat16))


def to_bf16(values):
    return lax.reduce_precision(values, exponent_bits=8, mantissa_bits=7).astype(jnp.bfloat16)


def short_causal(prior_rows, inputs, filter_taps):
    length = inputs.shape[0]
    padded = jnp.concatenate([prior_rows.astype(jnp.float32), inputs.astype(jnp.float32)], axis=0)
    summed = jnp.zeros(inputs.shape, jnp.float32)
    for offset in range(SHORT):
        summed = (
            summed + filter_taps[offset] * padded[SHORT - 1 - offset : SHORT - 1 - offset + length]
        )
    return summed


def short_reverse(grad_rows, next_rows, filter_taps):
    length = grad_rows.shape[0]
    padded = jnp.concatenate([grad_rows.astype(jnp.float32), next_rows.astype(jnp.float32)], axis=0)
    summed = jnp.zeros(grad_rows.shape, jnp.float32)
    for offset in range(SHORT):
        summed = summed + filter_taps[offset] * padded[offset : offset + length]
    return summed


def split_dot(spec, table, values):
    high = lax.reduce_precision(table, exponent_bits=8, mantissa_bits=7)
    low = (table - high).astype(jnp.bfloat16)
    lhs = jnp.einsum(spec, high.astype(jnp.bfloat16), values, preferred_element_type=jnp.float32)
    return lhs + jnp.einsum(spec, low, values, preferred_element_type=jnp.float32)


def cube_coefficients(size, index):
    terms = []
    shift = 1
    while shift < size:
        offset = (index % shift).astype(jnp.float32)
        terms += [jnp.float32(shift), offset, shift - 1 - offset]
        shift *= 2
    return terms


def cube_weights(factors, size, index):
    rounds = []
    shift = 1
    step = 0
    while shift < size:
        upper = (index & shift) != 0
        span, lead, trail = factors[step], factors[step + 1], factors[step + 2]
        one = jnp.ones_like(span)
        zero = jnp.zeros_like(span)
        keep = jnp.stack([jnp.where(upper, one, span), jnp.where(upper, span, one)])
        take = jnp.stack([jnp.where(upper, span, one), jnp.where(upper, one, span)])
        add = jnp.stack([jnp.where(upper, lead, zero), jnp.where(upper, zero, trail)])
        rounds.append((keep, take, add))
        shift *= 2
        step += 3
    return rounds


def cube_scan(window, rounds, axis, size, held):
    entering = jnp.zeros_like(window)
    shift = 1
    for keep, take, add in rounds:
        arrived = lax.ppermute(window, axis, [(source, source ^ shift) for source in range(size)])
        if shift == 1:
            held, arrived = lax.optimization_barrier((held, arrived))
        entering = entering + add * arrived
        window = keep * window + take * arrived
        shift *= 2
    return entering, window, held


def shards(inner, u_query, u_key, u_value, short_filter, decay_rate, residue, grad_out):
    block_len, channels = u_query.shape
    group_count = channels // GROUP
    rim_rows = jnp.stack(
        [
            u_query[block_len - SHORT + 1 :],
            u_key[block_len - SHORT + 1 :],
            u_value[block_len - SHORT + 1 :],
        ]
    )
    before = from_behind(rim_rows, ("zl", "xc"), 1)
    q_short = to_bf16(short_causal(before[0], u_query, short_filter[0]))
    k_short = to_bf16(short_causal(before[1], u_key, short_filter[1]))
    v_short = to_bf16(short_causal(before[2], u_value, short_filter[2]))
    product = rounded(k_short.astype(jnp.float32) * v_short.astype(jnp.float32))
    grad_conv = rounded(grad_out.astype(jnp.float32) * q_short.astype(jnp.float32))

    rates = decay_rate
    weights = residue * jnp.sqrt(-jnp.expm1(-2.0 * rates))
    lags = jnp.arange(block_len + 1).astype(jnp.float32)
    powers = jnp.exp(-rates[:, :, None] * lags)

    signal = product.reshape(block_len, group_count, GROUP)
    cotangent = grad_conv.reshape(block_len, group_count, GROUP)
    order = rates.shape[1]
    owner = (jnp.arange(channels) // GROUP)[None, :] == jnp.arange(group_count)[:, None]
    owner = owner.astype(jnp.float32)

    def own_block(full):
        return (full.reshape(group_count, order, channels) * owner[:, None, :]).sum(0)

    def spread(state):
        return (state[None] * owner[:, None, :]).reshape(group_count * order, channels)

    end_rows = powers[:, :, block_len - 1 :: -1].reshape(group_count * order, block_len)
    start_rows = powers[:, :, :block_len].reshape(group_count * order, block_len)
    end_state = own_block(split_dot("ks,sc->kc", end_rows, product))
    start_state = own_block(split_dot("ks,sc->kc", start_rows, grad_conv))
    decay_step = jnp.repeat(rates.T, GROUP, axis=1) * block_len
    member = lax.axis_index("xc")
    outer = lax.axis_size("zl")
    band = lax.axis_index("zl")
    place = member.astype(jnp.float32)
    inner_terms = cube_coefficients(inner, member)
    outer_terms = [inner * term for term in cube_coefficients(outer, band)]
    unit_terms = [place, inner - 1 - place, jnp.float32(1), jnp.float32(-1)]
    terms = jnp.stack(inner_terms + outer_terms + unit_terms)
    factors = jnp.exp(-decay_step[None] * terms[:, None, None])
    inner_rounds = cube_weights(factors, inner, member)
    outer_rounds = cube_weights(factors[len(inner_terms) :], outer, band)
    near, group, (rates, weights) = cube_scan(
        jnp.stack([end_state, start_state]), inner_rounds, "xc", inner, (rates, weights)
    )
    far, _, _ = cube_scan(group, outer_rounds, "zl", outer, ())
    entering = near[0] + factors[-4] * far[0]
    leaving = near[1] + factors[-3] * far[1]

    centred = jnp.arange(block_len).astype(jnp.float32) - block_len // 2
    falling = weights[:, None, :] * jnp.exp(-centred[None, :, None] * rates[:, None, :])
    rising = jnp.exp(centred[None, None, :] * rates[:, :, None])
    toeplitz = jnp.einsum("gtm,gms->gts", falling, rising, precision=precise)
    lower = jnp.arange(block_len)[:, None] >= jnp.arange(block_len)[None, :]
    toeplitz = jnp.where(lower[None], toeplitz, 0.0)
    local_conv = split_dot("gts,sgc->tgc", toeplitz, signal).reshape(block_len, channels)
    local_grad = split_dot("gts,tgc->sgc", toeplitz, cotangent).reshape(block_len, channels)
    lead_fwd = (weights[:, :, None] * powers[:, :, 1:]).reshape(group_count * order, block_len)
    lead_bwd = (weights[:, :, None] * powers[:, :, block_len:0:-1]).reshape(
        group_count * order, block_len
    )
    carried_conv = jnp.einsum("kt,kc->tc", lead_fwd, spread(entering), precision=precise)
    carried_grad = jnp.einsum("ks,kc->sc", lead_bwd, spread(leaving), precision=precise)
    conv_out = to_bf16(local_conv + carried_conv)
    grad_prod = to_bf16(local_grad + carried_grad)

    edge = SHORT - 1
    ahead = jnp.concatenate(
        [
            local_conv[:edge],
            local_grad[:edge],
            grad_out[:edge].astype(jnp.float32),
            k_short[:edge].astype(jnp.float32),
            v_short[:edge].astype(jnp.float32),
            start_state,
        ]
    )
    ahead = from_behind(ahead, ("zl", "xc"), -1)
    through = factors[-2] * entering + end_state
    beyond = (leaving - ahead[5 * edge :]) * factors[-1]
    next_conv = rounded(
        ahead[:edge]
        + jnp.einsum("kt,kc->tc", lead_fwd[:, :edge], spread(through), precision=precise)
    )
    next_grad = rounded(
        ahead[edge : 2 * edge]
        + jnp.einsum("ks,kc->sc", lead_bwd[:, :edge], spread(beyond), precision=precise)
    )
    next_rows = (
        rounded(ahead[2 * edge : 3 * edge] * next_conv.astype(jnp.float32)),
        rounded(next_grad.astype(jnp.float32) * ahead[4 * edge : 5 * edge]),
        rounded(next_grad.astype(jnp.float32) * ahead[3 * edge : 4 * edge]),
    )

    mixer_out = (q_short.astype(jnp.float32) * conv_out.astype(jnp.float32)).astype(jnp.bfloat16)
    grad_qshort = rounded(grad_out.astype(jnp.float32) * conv_out.astype(jnp.float32))
    grad_kshort = rounded(grad_prod.astype(jnp.float32) * v_short.astype(jnp.float32))
    grad_vshort = rounded(grad_prod.astype(jnp.float32) * k_short.astype(jnp.float32))
    grad_query = short_reverse(grad_qshort, next_rows[0], short_filter[0]).astype(jnp.bfloat16)
    grad_key = short_reverse(grad_kshort, next_rows[1], short_filter[1]).astype(jnp.bfloat16)
    grad_value = short_reverse(grad_vshort, next_rows[2], short_filter[2]).astype(jnp.bfloat16)
    return (mixer_out, grad_query, grad_key, grad_value)


def solution(mesh):
    ctx_count = mesh.shape["ctx"]
    inner = math.gcd(INNER, ctx_count)
    grid = Mesh(
        mesh.devices.reshape(ctx_count // inner, inner, mesh.shape["tp"]), ("zl", "xc", "tp")
    )
    rows = P(("zl", "xc"), "tp")
    return jax.shard_map(
        lambda *arrays: shards(inner, *arrays),
        mesh=grid,
        in_specs=(rows, rows, rows, P(None, None, "tp"), P("tp", None), P("tp", None), rows),
        out_specs=(rows, rows, rows, rows),
        check_vma=False,
    )
```

```python
import math

import jax
import jax.numpy as jnp
from jax import lax
from jax.sharding import Mesh, PartitionSpec as P

GROUP = 16
SHORT = 7
INNER = 8


precise = lax.Precision.HIGHEST


def from_behind(value, axis, steps):
    count = lax.axis_size(axis)
    leading, last = (max(0, -steps), min(count, count - steps))
    return lax.ppermute(value, axis, [(source, source + steps) for source in range(leading, last)])


def rounded(values):
    return lax.optimization_barrier(values.astype(jnp.bfloat16))


def to_bf16(values):
    return lax.reduce_precision(values, exponent_bits=8, mantissa_bits=7).astype(jnp.bfloat16)


def short_causal(prior_rows, inputs, filter_taps):
    length = inputs.shape[0]
    padded = jnp.concatenate([prior_rows.astype(jnp.float32), inputs.astype(jnp.float32)], axis=0)
    summed = jnp.zeros(inputs.shape, jnp.float32)
    for offset in range(SHORT):
        summed = (
            summed + filter_taps[offset] * padded[SHORT - 1 - offset : SHORT - 1 - offset + length]
        )
    return summed


def short_reverse(grad_rows, next_rows, filter_taps):
    length = grad_rows.shape[0]
    padded = jnp.concatenate([grad_rows.astype(jnp.float32), next_rows.astype(jnp.float32)], axis=0)
    summed = jnp.zeros(grad_rows.shape, jnp.float32)
    for offset in range(SHORT):
        summed = summed + filter_taps[offset] * padded[offset : offset + length]
    return summed


def split_dot(spec, table, values):
    high = lax.reduce_precision(table, exponent_bits=8, mantissa_bits=7)
    low = (table - high).astype(jnp.bfloat16)
    lhs = jnp.einsum(spec, high.astype(jnp.bfloat16), values, preferred_element_type=jnp.float32)
    return lhs + jnp.einsum(spec, low, values, preferred_element_type=jnp.float32)


def cube_coefficients(size, index):
    terms = []
    shift = 1
    while shift < size:
        offset = (index % shift).astype(jnp.float32)
        terms += [jnp.float32(shift), offset, shift - 1 - offset]
        shift *= 2
    return terms


def cube_weights(factors, size, index):
    rounds = []
    shift = 1
    step = 0
    while shift < size:
        upper = (index & shift) != 0
        span, lead, trail = factors[step], factors[step + 1], factors[step + 2]
        one = jnp.ones_like(span)
        zero = jnp.zeros_like(span)
        keep = jnp.stack([jnp.where(upper, one, span), jnp.where(upper, span, one)])
        take = jnp.stack([jnp.where(upper, span, one), jnp.where(upper, one, span)])
        add = jnp.stack([jnp.where(upper, lead, zero), jnp.where(upper, zero, trail)])
        rounds.append((keep, take, add))
        shift *= 2
        step += 3
    return rounds


def cube_scan(window, rounds, axis, size, held):
    entering = jnp.zeros_like(window)
    shift = 1
    for keep, take, add in rounds:
        arrived = lax.ppermute(window, axis, [(source, source ^ shift) for source in range(size)])
        if shift == 1:
            held, arrived = lax.optimization_barrier((held, arrived))
        entering = entering + add * arrived
        window = keep * window + take * arrived
        shift *= 2
    return entering, window, held


def shards(inner, u_query, u_key, u_value, short_filter, decay_rate, residue, grad_out):
    block_len, channels = u_query.shape
    group_count = channels // GROUP
    rim_rows = jnp.stack(
        [
            u_query[block_len - SHORT + 1 :],
            u_key[block_len - SHORT + 1 :],
            u_value[block_len - SHORT + 1 :],
        ]
    )
    before = from_behind(rim_rows, ("zl", "xc"), 1)
    q_short = to_bf16(short_causal(before[0], u_query, short_filter[0]))
    k_short = to_bf16(short_causal(before[1], u_key, short_filter[1]))
    v_short = to_bf16(short_causal(before[2], u_value, short_filter[2]))
    product = to_bf16(k_short.astype(jnp.float32) * v_short.astype(jnp.float32))
    grad_conv = to_bf16(grad_out.astype(jnp.float32) * q_short.astype(jnp.float32))

    rates = decay_rate
    weights = residue * jnp.sqrt(-jnp.expm1(-2.0 * rates))
    lags = jnp.arange(block_len + 1).astype(jnp.float32)
    powers = jnp.exp(-rates[:, :, None] * lags)

    signal = product.reshape(block_len, group_count, GROUP)
    cotangent = grad_conv.reshape(block_len, group_count, GROUP)
    order = rates.shape[1]
    owner = (jnp.arange(channels) // GROUP)[None, :] == jnp.arange(group_count)[:, None]
    owner = owner.astype(jnp.float32)

    def own_block(full):
        return (full.reshape(group_count, order, channels) * owner[:, None, :]).sum(0)

    def spread(state):
        return (state[None] * owner[:, None, :]).reshape(group_count * order, channels)

    end_rows = powers[:, :, block_len - 1 :: -1].reshape(group_count * order, block_len)
    start_rows = powers[:, :, :block_len].reshape(group_count * order, block_len)
    end_state = own_block(split_dot("ks,sc->kc", end_rows, product))
    start_state = own_block(split_dot("ks,sc->kc", start_rows, grad_conv))
    decay_step = jnp.repeat(rates.T, GROUP, axis=1) * block_len
    member = lax.axis_index("xc")
    outer = lax.axis_size("zl")
    band = lax.axis_index("zl")
    place = member.astype(jnp.float32)
    inner_terms = cube_coefficients(inner, member)
    outer_terms = [inner * term for term in cube_coefficients(outer, band)]
    unit_terms = [place, inner - 1 - place, jnp.float32(1), jnp.float32(-1)]
    terms = jnp.stack(inner_terms + outer_terms + unit_terms)
    factors = jnp.exp(-decay_step[None] * terms[:, None, None])
    inner_rounds = cube_weights(factors, inner, member)
    outer_rounds = cube_weights(factors[len(inner_terms) :], outer, band)
    near, group, (rates, weights) = cube_scan(
        jnp.stack([end_state, start_state]), inner_rounds, "xc", inner, (rates, weights)
    )
    far, _, _ = cube_scan(group, outer_rounds, "zl", outer, ())
    entering = near[0] + factors[-4] * far[0]
    leaving = near[1] + factors[-3] * far[1]

    centred = jnp.arange(block_len).astype(jnp.float32) - block_len // 2
    falling = weights[:, None, :] * jnp.exp(-centred[None, :, None] * rates[:, None, :])
    rising = jnp.exp(centred[None, None, :] * rates[:, :, None])
    toeplitz = jnp.einsum("gtm,gms->gts", falling, rising, precision=precise)
    lower = jnp.arange(block_len)[:, None] >= jnp.arange(block_len)[None, :]
    toeplitz = jnp.where(lower[None], toeplitz, 0.0)
    local_conv = split_dot("gts,sgc->tgc", toeplitz, signal).reshape(block_len, channels)
    local_grad = split_dot("gts,tgc->sgc", toeplitz, cotangent).reshape(block_len, channels)
    lead_fwd = (weights[:, :, None] * powers[:, :, 1:]).reshape(group_count * order, block_len)
    lead_bwd = (weights[:, :, None] * powers[:, :, block_len:0:-1]).reshape(
        group_count * order, block_len
    )
    carried_conv = jnp.einsum("kt,kc->tc", lead_fwd, spread(entering), precision=precise)
    carried_grad = jnp.einsum("ks,kc->sc", lead_bwd, spread(leaving), precision=precise)
    conv_out = to_bf16(local_conv + carried_conv)
    grad_prod = to_bf16(local_grad + carried_grad)

    edge = SHORT - 1
    ahead = jnp.concatenate(
        [
            local_conv[:edge],
            local_grad[:edge],
            grad_out[:edge].astype(jnp.float32),
            k_short[:edge].astype(jnp.float32),
            v_short[:edge].astype(jnp.float32),
            start_state,
        ]
    )
    ahead = from_behind(ahead, ("zl", "xc"), -1)
    through = factors[-2] * entering + end_state
    beyond = (leaving - ahead[5 * edge :]) * factors[-1]
    next_conv = rounded(
        ahead[:edge]
        + jnp.einsum("kt,kc->tc", lead_fwd[:, :edge], spread(through), precision=precise)
    )
    next_grad = rounded(
        ahead[edge : 2 * edge]
        + jnp.einsum("ks,kc->sc", lead_bwd[:, :edge], spread(beyond), precision=precise)
    )
    next_rows = (
        rounded(ahead[2 * edge : 3 * edge] * next_conv.astype(jnp.float32)),
        rounded(next_grad.astype(jnp.float32) * ahead[4 * edge : 5 * edge]),
        rounded(next_grad.astype(jnp.float32) * ahead[3 * edge : 4 * edge]),
    )

    mixer_out = (q_short.astype(jnp.float32) * conv_out.astype(jnp.float32)).astype(jnp.bfloat16)
    grad_qshort = rounded(grad_out.astype(jnp.float32) * conv_out.astype(jnp.float32))
    grad_kshort = rounded(grad_prod.astype(jnp.float32) * v_short.astype(jnp.float32))
    grad_vshort = rounded(grad_prod.astype(jnp.float32) * k_short.astype(jnp.float32))
    grad_query = short_reverse(grad_qshort, next_rows[0], short_filter[0]).astype(jnp.bfloat16)
    grad_key = short_reverse(grad_kshort, next_rows[1], short_filter[1]).astype(jnp.bfloat16)
    grad_value = short_reverse(grad_vshort, next_rows[2], short_filter[2]).astype(jnp.bfloat16)
    return (mixer_out, grad_query, grad_key, grad_value)


def solution(mesh):
    ctx_count = mesh.shape["ctx"]
    inner = math.gcd(INNER, ctx_count)
    grid = Mesh(
        mesh.devices.reshape(ctx_count // inner, inner, mesh.shape["tp"]), ("zl", "xc", "tp")
    )
    rows = P(("zl", "xc"), "tp")
    return jax.shard_map(
        lambda *arrays: shards(inner, *arrays),
        mesh=grid,
        in_specs=(rows, rows, rows, P(None, None, "tp"), P("tp", None), P("tp", None), rows),
        out_specs=(rows, rows, rows, rows),
        check_vma=False,
    )
```
